512 devices in a mesh: ctx: 64 (over x, z_lo, core), head: 8 (over y, z_hi).
Axes of the slice: x: 4, y: 4, z: 16 (z_hi: 2, z_lo: 8; z = z_hi * 8 + z_lo), core: 2. Of those that a mesh axis runs over, the one named last changes fastest.
Arguments:
- queries: bfloat16 [16384, 2048], P('ctx', 'head'), may hold values from -40 to 40
- keys: bfloat16 [16384, 2048], P('ctx', 'head'), may hold values from -4 to 4
- values: bfloat16 [16384, 2048], P('ctx', 'head'), may hold values from -5 to 5
- selected: int32 [16, 512, 3], P('head', 'ctx'), may hold values from 0 to 63, as said below
- out_weight: bfloat16 [2048, 2048], P(None, 'head'), may hold values from -0.125 to 0.125
Outputs:
- projected: bfloat16 [16384, 2048], P('ctx', 'head')
The draws below stay inside these ranges and needn't reach their ends.
Inputs may be any that keep to these rules, and one draw needn't show every extreme that they name: `selected`: entry 0 of a tile's selection is its own block; entries 1 and 2 are two different earlier blocks, or both the own block where no earlier block is chosen for the tile (one earlier block and the own block in the second key block). For each head, the tiles of one key block name any one other block at most 2 times, and exactly 2 times for every block they name, from the third key block on.
All inputs are finite; a program needn't handle non-finite values.
Results may differ from the reference program's by a relative error of at most 0.0054.
Values may be sent and summed in bfloat16 or wider, within the bound.
No kernel may reach another device: no remote copies, remote signals or barrier semaphores. Data moves between devices by JAX's collectives and lax.ppermute only.
A program may use at most 64 MiB of HBM per device.

```python
import jax
import jax.numpy as jnp
from jax import lax

HEADS = 16
HEAD_DIM = 128
D = 2048
TILE = 32
TOPK = 3
BLOCK = 256
CONTEXT = 16384


def paired_fields(key):
    shape = (CONTEXT, HEADS * HEAD_DIM)
    keys = jnp.clip(jax.random.normal(jax.random.fold_in(key, 11), shape, jnp.float32), -4.0, 4.0)
    queries = jnp.clip(jax.random.normal(jax.random.fold_in(key, 12), shape, jnp.float32), -4.0, 4.0)
    return (keys, queries)


def draw_keys(key, part):
    return paired_fields(key)[0].astype(jnp.bfloat16)


def draw_queries(key, part):
    return paired_fields(key)[1].astype(jnp.bfloat16)


def draw_selected(key, part):
    tile_quantity = CONTEXT // BLOCK
    nt = BLOCK // TILE
    unscaled_logits = jax.random.randint(jax.random.fold_in(key, 21), (HEADS, tile_quantity, tile_quantity), 0, 4096)
    anchor_tile = jax.random.randint(jax.random.fold_in(key, 22), (HEADS, tile_quantity, 1), 0, 8192)
    key_position_number = jnp.arange(tile_quantity, dtype=jnp.int32)
    holder_rank = key_position_number[:, None]
    logit_increment = jnp.where(key_position_number[None, None, :] == 0, anchor_tile, 0) + jnp.where(key_position_number[None, :] == holder_rank - 1, 3000, 0)[None]
    preceding_filter = (key_position_number[None, :] < holder_rank)[None]
    group_relevance = jnp.where(preceding_filter, (unscaled_logits + logit_increment) * tile_quantity + key_position_number, -1 - key_position_number)
    order = jnp.argsort(-group_relevance, axis=-1).astype(jnp.int32)
    count = jnp.minimum(key_position_number, nt)
    safe = jnp.maximum(count, 1)
    slots = jnp.arange(nt, dtype=jnp.int32)
    first_pos = jnp.broadcast_to((slots[None, :] % safe[:, None])[None], (HEADS, tile_quantity, nt))
    second_pos = jnp.broadcast_to(((slots[None, :] + 1) % safe[:, None])[None], (HEADS, tile_quantity, nt))
    first = jnp.take_along_axis(order, first_pos, axis=-1)
    second = jnp.take_along_axis(order, second_pos, axis=-1)
    own = jnp.broadcast_to(holder_rank[None], (HEADS, tile_quantity, nt))
    live = (slots[None, :] < count[:, None])[None]
    pick_one = jnp.where(live, first, own)
    pick_two = jnp.where(jnp.logical_and(live, (count[:, None] >= 2)[None]), second, own)
    ranks_raw = jax.random.randint(jax.random.fold_in(key, 23), (HEADS, tile_quantity, nt), 0, 2 ** 20) * nt + slots
    ranks = jnp.argsort(jnp.argsort(ranks_raw, axis=-1), axis=-1).astype(jnp.int32)
    pick_one = jnp.take_along_axis(pick_one, ranks, axis=-1)
    pick_two = jnp.take_along_axis(pick_two, ranks, axis=-1)
    chosen = jnp.stack([own, pick_one, pick_two], axis=-1)
    return chosen.reshape(HEADS, tile_quantity * nt, TOPK).astype(jnp.int32)


def shard_levels(stream_key, shape, pieces, smallest, largest):
    gain = 1.0
    for axis_at, blocks in pieces:
        draws = jax.random.uniform(jax.random.fold_in(jax.random.fold_in(stream_key, 6), axis_at), (blocks,), jnp.float32, smallest / len(pieces), largest / len(pieces))
        gain = gain * jnp.repeat(jnp.exp(draws), shape[axis_at] // blocks).reshape((-1,) + (1,) * (len(shape) - 1 - axis_at))
    return gain


def centred(stream_key, extent, spread, reach, cuts=(), kind=jnp.bfloat16):
    result = jax.random.normal(stream_key, extent, jnp.float32) * spread
    if len(cuts) > 0:
        result = shard_levels(stream_key, extent, cuts, -0.22, 0.18) * result
    return jnp.clip(result, min=-reach, max=reach).astype(kind)


def setup_inputs(seed: int = 0) -> dict:
    arg_keys = jax.random.split(jax.random.key(seed), 6)
    return {
        "queries": draw_queries(jax.random.fold_in(arg_keys[5], 71), 0),
        "keys": draw_keys(jax.random.fold_in(arg_keys[5], 71), 0),
        "values": centred(arg_keys[2], (CONTEXT, HEADS * HEAD_DIM), 1.0, 5.0, ((0, 64), (1, 8))),
        "selected": draw_selected(jax.random.fold_in(arg_keys[5], 71), 0),
        "out_weight": centred(arg_keys[4], (HEADS * HEAD_DIM, D), (HEADS * HEAD_DIM) ** -0.5, 0.125, ((1, 8),)),
    }


def reference(queries, keys, values, selected, out_weight):
    tile_quantity = CONTEXT // BLOCK
    nt = BLOCK // TILE
    scale = HEAD_DIM ** -0.5
    qb = queries.reshape(tile_quantity, nt, TILE, HEADS, HEAD_DIM)
    kb = keys.reshape(tile_quantity, BLOCK, HEADS, HEAD_DIM)
    vb = values.reshape(tile_quantity, BLOCK, HEADS, HEAD_DIM)
    sb = jnp.transpose(selected.reshape(HEADS, tile_quantity, nt, TOPK), (1, 0, 2, 3))
    pos = jnp.arange(BLOCK, dtype=jnp.int32)
    causal = (pos[:, None] >= pos[None, :]).reshape(nt, TILE, BLOCK)
    head_ids = jnp.arange(HEADS, dtype=jnp.int32)

    def finish(scores, vals_f, form):
        top = jnp.max(scores, axis=-1)
        prob = jnp.exp(scores - top[..., None])
        total = jnp.sum(prob, axis=-1)
        weights = prob.astype(jnp.bfloat16).astype(jnp.float32)
        part = jnp.einsum(form, weights, vals_f) / total[..., None]
        return part, top + jnp.log(total)

    def one_block(b):
        query = qb[b].astype(jnp.float32)
        own_k = kb[b].astype(jnp.float32)
        own_v = vb[b].astype(jnp.float32)
        s0 = jnp.einsum('ntha,kha->hntk', query, own_k) * scale
        s0 = jnp.where(causal[None], s0, jnp.float32(-1e30))
        out0, lse0 = finish(s0, own_v, 'hntk,kha->hnta')
        top = lse0
        kept = []
        for r in range(1, TOPK):
            picks = sb[b, :, :, r]
            sel_k = kb[picks, :, head_ids[:, None], :].astype(jnp.float32)
            sel_v = vb[picks, :, head_ids[:, None], :].astype(jnp.float32)
            s = jnp.einsum('ntha,hnka->hntk', query, sel_k) * scale
            part, lse = finish(s, sel_v, 'hntk,hnka->hnta')
            valid = (picks != b)[:, :, None]
            kept.append((part, lse, valid))
            top = jnp.maximum(top, jnp.where(valid, lse, lse0))
        w0 = jnp.exp(lse0 - top)
        num = w0[..., None] * out0
        den = w0
        for part, lse, valid in kept:
            w = jnp.exp(jnp.where(valid, lse - top, jnp.float32(-1e30)))
            num = num + w[..., None] * part
            den = den + w
        att = num / den[..., None]
        att = jnp.transpose(att, (1, 2, 0, 3)).reshape(BLOCK, HEADS * HEAD_DIM)
        return att.astype(jnp.bfloat16)

    attention = lax.map(one_block, jnp.arange(tile_quantity, dtype=jnp.int32))

    def project(rows):
        return jnp.dot(rows, out_weight, preferred_element_type=jnp.float32).astype(jnp.bfloat16)

    projected = lax.map(project, attention)
    return projected.reshape(CONTEXT, D)
```

```python
import jax
import jax.numpy as jnp
from jax import lax
from jax.sharding import PartitionSpec as P

CAP = 2
LSE_ROWS = 16


def split_bf16(x):
    hi = lax.reduce_precision(x, exponent_bits=8, mantissa_bits=7)
    rest = x - hi
    mid = lax.reduce_precision(rest, exponent_bits=8, mantissa_bits=7)
    lo = rest - mid
    return jnp.stack([hi, mid, lo]).astype(jnp.bfloat16)


def join_bf16(parts):
    parts = parts.astype(jnp.float32)
    return parts[0] + (parts[1] + parts[2])


def softmax_pv(scores, vals):
    top = jnp.max(scores, axis=-1)
    prob = jnp.exp(scores - top[..., None])
    total = jnp.sum(prob, axis=-1)
    part = jnp.einsum(
        "hrk,khd->hrd", prob.astype(jnp.bfloat16), vals, preferred_element_type=jnp.float32
    )
    return part / total[..., None], top + jnp.log(total)


def local(queries, keys, values, selected, out_weight):
    heads_loc = selected.shape[0]
    tiles = selected.shape[1]
    tokens_here = queries.shape[0]
    width = queries.shape[1] // heads_loc
    tile_rows = tokens_here // tiles
    sources = lax.axis_size("ctx")
    mine = lax.axis_index("ctx")
    scale = width ** (-0.5)
    quer_three = queries.reshape(tokens_here, heads_loc, width)
    keys_three = keys.reshape(tokens_here, heads_loc, width)
    vals_three = values.reshape(tokens_here, heads_loc, width)

    pos = jnp.arange(tokens_here, dtype=jnp.int32)
    own_scores = (
        jnp.einsum("rhd,khd->hrk", quer_three, keys_three, preferred_element_type=jnp.float32)
        * scale
    )
    own_scores = jnp.where((pos[:, None] >= pos[None, :])[None], own_scores, jnp.float32(-1e30))
    own_out, own_lse = softmax_pv(own_scores, vals_three)
    own_out = own_out.reshape(heads_loc, tiles, tile_rows, width)
    own_lse = own_lse.reshape(heads_loc, tiles, tile_rows)

    picks = selected[:, :, 1:]
    valid = picks != mine
    target = jnp.where(valid, picks, sources)
    onehot = (target[..., None] == jnp.arange(sources, dtype=jnp.int32)).astype(jnp.int32)
    flat_hot = onehot.reshape(heads_loc, tiles * 2, sources)
    before = jnp.cumsum(flat_hot, axis=1) - flat_hot
    slot = jnp.sum(before * flat_hot, axis=-1).reshape(heads_loc, tiles, 2)
    head_idx = jnp.broadcast_to(
        jnp.arange(heads_loc, dtype=jnp.int32)[:, None, None], (heads_loc, tiles, 2)
    )
    query_src = jnp.transpose(quer_three.reshape(tiles, tile_rows, heads_loc, width), (2, 0, 1, 3))
    query_pairs = jnp.broadcast_to(query_src[:, :, None], (heads_loc, tiles, 2, tile_rows, width))
    send_q = jnp.zeros((sources, CAP, heads_loc, tile_rows, width), jnp.bfloat16)
    send_q = send_q.at[target, slot, head_idx].set(query_pairs, mode="drop")
    got_rows = lax.all_to_all(send_q, "ctx", split_axis=0, concat_axis=0, tiled=True)

    got_q = jnp.transpose(got_rows, (2, 0, 1, 3, 4)).reshape(
        heads_loc, sources * CAP * tile_rows, width
    )
    got_scores = (
        jnp.einsum("hrd,khd->hrk", got_q, keys_three, preferred_element_type=jnp.float32) * scale
    )
    part, lse = softmax_pv(got_scores, vals_three)
    part = jnp.transpose(
        part.reshape(heads_loc, sources, CAP, tile_rows, width), (1, 2, 0, 3, 4)
    ).reshape(sources, CAP * heads_loc * tile_rows, width)
    lse = jnp.transpose(lse.reshape(heads_loc, sources, CAP, tile_rows), (1, 2, 0, 3)).reshape(
        sources, CAP * heads_loc * tile_rows
    )
    lse_parts = jnp.transpose(split_bf16(lse), (1, 0, 2)).reshape(sources, -1, width)
    pad = -lse_parts.shape[1] % LSE_ROWS
    back = jnp.concatenate(
        [
            part.astype(jnp.bfloat16),
            lse_parts,
            jnp.zeros((sources, pad, width), jnp.bfloat16),
        ],
        axis=1,
    )
    got_back = lax.all_to_all(back, "ctx", split_axis=0, concat_axis=0, tiled=True)
    rows_part = CAP * heads_loc * tile_rows
    got_out = got_back[:, :rows_part].reshape(sources, CAP, heads_loc, tile_rows, width)
    got_lse = join_bf16(
        jnp.transpose(
            got_back[:, rows_part : rows_part + lse_parts.shape[1]].reshape(sources, 3, rows_part),
            (1, 0, 2),
        )
    ).reshape(sources, CAP, heads_loc, tile_rows)

    clipped = jnp.clip(target, 0, sources - 1)
    pick_out = got_out[clipped, slot, head_idx].astype(jnp.float32)
    pick_lse = got_lse[clipped, slot, head_idx]
    keep = valid[..., None]
    top = jnp.maximum(own_lse, jnp.max(jnp.where(keep, pick_lse, own_lse[:, :, None]), axis=2))
    own_w = jnp.exp(own_lse - top)
    pick_w = jnp.exp(jnp.where(keep, pick_lse - top[:, :, None], jnp.float32(-1e30)))
    numer = own_w[..., None] * own_out + jnp.sum(pick_w[..., None] * pick_out, axis=2)
    denom = own_w + jnp.sum(pick_w, axis=2)
    attention = jnp.transpose(numer / denom[..., None], (1, 2, 0, 3)).reshape(
        tokens_here, heads_loc * width
    )
    attention = attention.astype(jnp.bfloat16)
    projected = jnp.dot(
        lax.all_gather(attention, "head", axis=1, tiled=True),
        out_weight,
        preferred_element_type=jnp.float32,
    )
    return projected.astype(jnp.bfloat16)


def solution(mesh):
    return jax.shard_map(
        local,
        mesh=mesh,
        in_specs=(
            P("ctx", "head"),
            P("ctx", "head"),
            P("ctx", "head"),
            P("head", "ctx", None),
            P(None, "head"),
        ),
        out_specs=P("ctx", "head"),
        check_vma=False,
    )
```

```python
import jax
import jax.numpy as jnp
from jax import lax
from jax.sharding import Mesh, PartitionSpec as P

CAP = 2
LSE_ROWS = 16


def split_bf16(x):
    hi = lax.reduce_precision(x, exponent_bits=8, mantissa_bits=7)
    rest = x - hi
    mid = lax.reduce_precision(rest, exponent_bits=8, mantissa_bits=7)
    lo = rest - mid
    return jnp.stack([hi, mid, lo]).astype(jnp.bfloat16)


def join_bf16(parts):
    parts = parts.astype(jnp.float32)
    return parts[0] + (parts[1] + parts[2])


def softmax_pv(scores, vals):
    top = jnp.max(scores, axis=-1)
    prob = jnp.exp(scores - top[..., None])
    total = jnp.sum(prob, axis=-1)
    part = jnp.einsum(
        "hrk,khd->hrd", prob.astype(jnp.bfloat16), vals, preferred_element_type=jnp.float32
    )
    return part / total[..., None], top + jnp.log(total)


def local(queries, keys, values, selected, out_weight):
    heads_loc = selected.shape[0]
    tiles = selected.shape[1]
    tokens_here = queries.shape[0]
    width = queries.shape[1] // heads_loc
    tile_rows = tokens_here // tiles
    sources = lax.axis_size("ctx")
    mine = lax.axis_index("ctx")
    scale = width ** (-0.5)
    quer_three = queries.reshape(tokens_here, heads_loc, width)
    keys_three = keys.reshape(tokens_here, heads_loc, width)
    vals_three = values.reshape(tokens_here, heads_loc, width)

    pos = jnp.arange(tokens_here, dtype=jnp.int32)
    own_scores = (
        jnp.einsum("rhd,khd->hrk", quer_three, keys_three, preferred_element_type=jnp.float32)
        * scale
    )
    own_scores = jnp.where((pos[:, None] >= pos[None, :])[None], own_scores, jnp.float32(-1e30))
    own_out, own_lse = softmax_pv(own_scores, vals_three)
    own_out = own_out.reshape(heads_loc, tiles, tile_rows, width)
    own_lse = own_lse.reshape(heads_loc, tiles, tile_rows)

    picks = selected[:, :, 1:]
    valid = picks != mine
    target = jnp.where(valid, picks, sources)
    onehot = (target[..., None] == jnp.arange(sources, dtype=jnp.int32)).astype(jnp.int32)
    flat_hot = onehot.reshape(heads_loc, tiles * 2, sources)
    before = jnp.cumsum(flat_hot, axis=1) - flat_hot
    slot = jnp.sum(before * flat_hot, axis=-1).reshape(heads_loc, tiles, 2)
    head_idx = jnp.broadcast_to(
        jnp.arange(heads_loc, dtype=jnp.int32)[:, None, None], (heads_loc, tiles, 2)
    )
    query_src = jnp.transpose(quer_three.reshape(tiles, tile_rows, heads_loc, width), (2, 0, 1, 3))
    query_pairs = jnp.broadcast_to(query_src[:, :, None], (heads_loc, tiles, 2, tile_rows, width))
    send_q = jnp.zeros((sources, CAP, heads_loc, tile_rows, width), jnp.bfloat16)
    send_q = send_q.at[target, slot, head_idx].set(query_pairs, mode="drop")
    got_rows = lax.all_to_all(send_q, "ctx", split_axis=0, concat_axis=0, tiled=True)

    got_q = jnp.transpose(got_rows, (2, 0, 1, 3, 4)).reshape(
        heads_loc, sources * CAP * tile_rows, width
    )
    got_scores = (
        jnp.einsum("hrd,khd->hrk", got_q, keys_three, preferred_element_type=jnp.float32) * scale
    )
    part, lse = softmax_pv(got_scores, vals_three)
    part = jnp.transpose(
        part.reshape(heads_loc, sources, CAP, tile_rows, width), (1, 2, 0, 3, 4)
    ).reshape(sources, CAP * heads_loc * tile_rows, width)
    lse = jnp.transpose(lse.reshape(heads_loc, sources, CAP, tile_rows), (1, 2, 0, 3)).reshape(
        sources, CAP * heads_loc * tile_rows
    )
    lse_parts = jnp.transpose(split_bf16(lse), (1, 0, 2)).reshape(sources, -1, width)
    pad = -lse_parts.shape[1] % LSE_ROWS
    back = jnp.concatenate(
        [
            part.astype(jnp.bfloat16),
            lse_parts,
            jnp.zeros((sources, pad, width), jnp.bfloat16),
        ],
        axis=1,
    )
    got_back = lax.all_to_all(back, "ctx", split_axis=0, concat_axis=0, tiled=True)
    rows_part = CAP * heads_loc * tile_rows
    got_out = got_back[:, :rows_part].reshape(sources, CAP, heads_loc, tile_rows, width)
    got_lse = join_bf16(
        jnp.transpose(
            got_back[:, rows_part : rows_part + lse_parts.shape[1]].reshape(sources, 3, rows_part),
            (1, 0, 2),
        )
    ).reshape(sources, CAP, heads_loc, tile_rows)

    clipped = jnp.clip(target, 0, sources - 1)
    pick_out = got_out[clipped, slot, head_idx].astype(jnp.float32)
    pick_lse = got_lse[clipped, slot, head_idx]
    keep = valid[..., None]
    top = jnp.maximum(own_lse, jnp.max(jnp.where(keep, pick_lse, own_lse[:, :, None]), axis=2))
    own_w = jnp.exp(own_lse - top)
    pick_w = jnp.exp(jnp.where(keep, pick_lse - top[:, :, None], jnp.float32(-1e30)))
    numer = own_w[..., None] * own_out + jnp.sum(pick_w[..., None] * pick_out, axis=2)
    denom = own_w + jnp.sum(pick_w, axis=2)
    attention = jnp.transpose(numer / denom[..., None], (1, 2, 0, 3)).reshape(
        tokens_here, heads_loc * width
    )
    attention = attention.astype(jnp.bfloat16)
    gathered = lax.all_gather(attention, "zh", axis=1, tiled=True)
    gathered = lax.all_gather(gathered, "y", axis=1, tiled=True)
    projected = jnp.dot(
        gathered,
        out_weight,
        preferred_element_type=jnp.float32,
    )
    return projected.astype(jnp.bfloat16)


def solution(mesh):
    ctx_n, head_n = mesh.devices.shape
    split = Mesh(mesh.devices.reshape(ctx_n, head_n // 2, 2), ("ctx", "y", "zh"))
    head = ("y", "zh")
    return jax.shard_map(
        local,
        mesh=split,
        in_specs=(
            P("ctx", head),
            P("ctx", head),
            P("ctx", head),
            P(head, "ctx", None),
            P(None, head),
        ),
        out_specs=P("ctx", head),
        check_vma=False,
    )
```

```python
import jax
import jax.numpy as jnp
from jax import lax
from jax.sharding import Mesh, PartitionSpec as P

CAP = 2
LSE_ROWS = 16


def split_bf16(x):
    hi = lax.reduce_precision(x, exponent_bits=8, mantissa_bits=7)
    rest = x - hi
    mid = lax.reduce_precision(rest, exponent_bits=8, mantissa_bits=7)
    lo = rest - mid
    return jnp.stack([hi, mid, lo]).astype(jnp.bfloat16)


def join_bf16(parts):
    parts = parts.astype(jnp.float32)
    return parts[0] + (parts[1] + parts[2])


def softmax_pv(scores, vals):
    top = jnp.max(scores, axis=-1)
    prob = jnp.exp(scores - top[..., None])
    total = jnp.sum(prob, axis=-1)
    part = jnp.einsum(
        "hrk,khd->hrd", prob.astype(jnp.bfloat16), vals, preferred_element_type=jnp.float32
    )
    return part / total[..., None], top + jnp.log(total)


def local(queries, keys, values, selected, out_weight):
    heads_loc = selected.shape[0]
    tiles = selected.shape[1]
    tokens_here = queries.shape[0]
    width = queries.shape[1] // heads_loc
    tile_rows = tokens_here // tiles
    sources = lax.axis_size("ctx")
    mine = lax.axis_index("ctx")
    scale = width ** (-0.5)
    quer_three = queries.reshape(tokens_here, heads_loc, width)
    keys_three = keys.reshape(tokens_here, heads_loc, width)
    vals_three = values.reshape(tokens_here, heads_loc, width)

    pos = jnp.arange(tokens_here, dtype=jnp.int32)
    own_scores = (
        jnp.einsum("rhd,khd->hrk", quer_three, keys_three, preferred_element_type=jnp.float32)
        * scale
    )
    own_scores = jnp.where((pos[:, None] >= pos[None, :])[None], own_scores, jnp.float32(-1e30))
    own_out, own_lse = softmax_pv(own_scores, vals_three)
    own_out = own_out.reshape(heads_loc, tiles, tile_rows, width)
    own_lse = own_lse.reshape(heads_loc, tiles, tile_rows)

    picks = selected[:, :, 1:]
    valid = picks != mine
    target = jnp.where(valid, picks, sources)
    onehot = (target[..., None] == jnp.arange(sources, dtype=jnp.int32)).astype(jnp.int32)
    flat_hot = onehot.reshape(heads_loc, tiles * 2, sources)
    before = jnp.cumsum(flat_hot, axis=1) - flat_hot
    slot = jnp.sum(before * flat_hot, axis=-1).reshape(heads_loc, tiles, 2)
    head_idx = jnp.broadcast_to(
        jnp.arange(heads_loc, dtype=jnp.int32)[:, None, None], (heads_loc, tiles, 2)
    )
    query_src = jnp.transpose(quer_three.reshape(tiles, tile_rows, heads_loc, width), (2, 0, 1, 3))
    query_pairs = jnp.broadcast_to(query_src[:, :, None], (heads_loc, tiles, 2, tile_rows, width))
    shift = jnp.where(valid, mine - picks, 0)
    send_q = jnp.zeros((sources, CAP, heads_loc, tile_rows, width), jnp.bfloat16)
    send_q = send_q.at[jnp.where(valid, shift, sources), slot, head_idx].set(
        query_pairs, mode="drop"
    )
    got_rows = jnp.stack(
        [jnp.zeros_like(send_q[0])]
        + [
            lax.ppermute(send_q[s], "ctx", [(b, b - s) for b in range(s, sources)])
            for s in range(1, sources)
        ]
    )

    got_q = jnp.transpose(got_rows, (2, 0, 1, 3, 4)).reshape(
        heads_loc, sources * CAP * tile_rows, width
    )
    got_scores = (
        jnp.einsum("hrd,khd->hrk", got_q, keys_three, preferred_element_type=jnp.float32) * scale
    )
    part, lse = softmax_pv(got_scores, vals_three)
    part = jnp.transpose(
        part.reshape(heads_loc, sources, CAP, tile_rows, width), (1, 2, 0, 3, 4)
    ).reshape(sources, CAP * heads_loc * tile_rows, width)
    lse = jnp.transpose(lse.reshape(heads_loc, sources, CAP, tile_rows), (1, 2, 0, 3)).reshape(
        sources, CAP * heads_loc * tile_rows
    )
    lse_parts = jnp.transpose(split_bf16(lse), (1, 0, 2)).reshape(sources, -1, width)
    pad = -lse_parts.shape[1] % LSE_ROWS
    back = jnp.concatenate(
        [
            part.astype(jnp.bfloat16),
            lse_parts,
            jnp.zeros((sources, pad, width), jnp.bfloat16),
        ],
        axis=1,
    )
    got_back = jnp.stack(
        [jnp.zeros_like(back[0])]
        + [
            lax.ppermute(back[s], "ctx", [(d, d + s) for d in range(0, sources - s)])
            for s in range(1, sources)
        ]
    )
    rows_part = CAP * heads_loc * tile_rows
    got_out = got_back[:, :rows_part].reshape(sources, CAP, heads_loc, tile_rows, width)
    got_lse = join_bf16(
        jnp.transpose(
            got_back[:, rows_part : rows_part + lse_parts.shape[1]].reshape(sources, 3, rows_part),
            (1, 0, 2),
        )
    ).reshape(sources, CAP, heads_loc, tile_rows)

    pick_out = got_out[shift, slot, head_idx].astype(jnp.float32)
    pick_lse = got_lse[shift, slot, head_idx]
    keep = valid[..., None]
    top = jnp.maximum(own_lse, jnp.max(jnp.where(keep, pick_lse, own_lse[:, :, None]), axis=2))
    own_w = jnp.exp(own_lse - top)
    pick_w = jnp.exp(jnp.where(keep, pick_lse - top[:, :, None], jnp.float32(-1e30)))
    numer = own_w[..., None] * own_out + jnp.sum(pick_w[..., None] * pick_out, axis=2)
    denom = own_w + jnp.sum(pick_w, axis=2)
    attention = jnp.transpose(numer / denom[..., None], (1, 2, 0, 3)).reshape(
        tokens_here, heads_loc * width
    )
    attention = attention.astype(jnp.bfloat16)
    gathered = lax.all_gather(attention, "zh", axis=1, tiled=True)
    gathered = lax.all_gather(gathered, "y", axis=1, tiled=True)
    projected = jnp.dot(
        gathered,
        out_weight,
        preferred_element_type=jnp.float32,
    )
    return projected.astype(jnp.bfloat16)


def solution(mesh):
    ctx_n, head_n = mesh.devices.shape
    split = Mesh(mesh.devices.reshape(ctx_n, head_n // 2, 2), ("ctx", "y", "zh"))
    head = ("y", "zh")
    return jax.shard_map(
        local,
        mesh=split,
        in_specs=(
            P("ctx", head),
            P("ctx", head),
            P("ctx", head),
            P(head, "ctx", None),
            P(None, head),
        ),
        out_specs=P("ctx", head),
        check_vma=False,
    )
```

```python
import jax
import jax.numpy as jnp
from jax import lax
from jax.sharding import Mesh, PartitionSpec as P

CAP = 2
LSE_ROWS = 16


def split_bf16(x):
    hi = lax.reduce_precision(x, exponent_bits=8, mantissa_bits=7)
    rest = x - hi
    mid = lax.reduce_precision(rest, exponent_bits=8, mantissa_bits=7)
    lo = rest - mid
    return jnp.stack([hi, mid, lo]).astype(jnp.bfloat16)


def join_bf16(parts):
    parts = parts.astype(jnp.float32)
    return parts[0] + (parts[1] + parts[2])


def softmax_pv(scores, vals):
    top = jnp.max(scores, axis=-1)
    prob = jnp.exp(scores - top[..., None])
    total = jnp.sum(prob, axis=-1)
    part = jnp.einsum(
        "hrk,khd->hrd", prob.astype(jnp.bfloat16), vals, preferred_element_type=jnp.float32
    )
    return part / total[..., None], top + jnp.log(total)


def local(queries, keys, values, selected, out_weight):
    heads_loc = selected.shape[0]
    tiles = selected.shape[1]
    tokens_here = queries.shape[0]
    width = queries.shape[1] // heads_loc
    tile_rows = tokens_here // tiles
    sources = lax.axis_size("ctx")
    mine = lax.axis_index("ctx")
    scale = width ** (-0.5)
    quer_three = queries.reshape(tokens_here, heads_loc, width)
    keys_three = keys.reshape(tokens_here, heads_loc, width)
    vals_three = values.reshape(tokens_here, heads_loc, width)

    pos = jnp.arange(tokens_here, dtype=jnp.int32)
    own_scores = (
        jnp.einsum("rhd,khd->hrk", quer_three, keys_three, preferred_element_type=jnp.float32)
        * scale
    )
    own_scores = jnp.where((pos[:, None] >= pos[None, :])[None], own_scores, jnp.float32(-1e30))
    own_out, own_lse = softmax_pv(own_scores, vals_three)
    own_out = own_out.reshape(heads_loc, tiles, tile_rows, width)
    own_lse = own_lse.reshape(heads_loc, tiles, tile_rows)

    picks = selected[:, :, 1:]
    valid = picks != mine
    target = jnp.where(valid, picks, sources)
    onehot = (target[..., None] == jnp.arange(sources, dtype=jnp.int32)).astype(jnp.int32)
    flat_hot = onehot.reshape(heads_loc, tiles * 2, sources)
    before = jnp.cumsum(flat_hot, axis=1) - flat_hot
    slot = jnp.sum(before * flat_hot, axis=-1).reshape(heads_loc, tiles, 2)
    head_idx = jnp.broadcast_to(
        jnp.arange(heads_loc, dtype=jnp.int32)[:, None, None], (heads_loc, tiles, 2)
    )
    query_src = jnp.transpose(quer_three.reshape(tiles, tile_rows, heads_loc, width), (2, 0, 1, 3))
    query_pairs = jnp.broadcast_to(query_src[:, :, None], (heads_loc, tiles, 2, tile_rows, width))
    send_q = jnp.zeros((sources, CAP, heads_loc, tile_rows, width), jnp.bfloat16)
    send_q = send_q.at[target, slot, head_idx].set(query_pairs, mode="drop")
    got_rows = lax.all_to_all(send_q, "ctx", split_axis=0, concat_axis=0, tiled=True)

    got_q = jnp.transpose(got_rows, (2, 0, 1, 3, 4)).reshape(
        heads_loc, sources * CAP * tile_rows, width
    )
    got_scores = (
        jnp.einsum("hrd,khd->hrk", got_q, keys_three, preferred_element_type=jnp.float32) * scale
    )
    part, lse = softmax_pv(got_scores, vals_three)
    part = jnp.transpose(
        part.reshape(heads_loc, sources, CAP, tile_rows, width), (1, 2, 0, 3, 4)
    ).reshape(sources, CAP * heads_loc * tile_rows, width)
    lse = jnp.transpose(lse.reshape(heads_loc, sources, CAP, tile_rows), (1, 2, 0, 3)).reshape(
        sources, CAP * heads_loc * tile_rows
    )
    lse_parts = jnp.transpose(split_bf16(lse), (1, 0, 2)).reshape(sources, -1, width)
    pad = -lse_parts.shape[1] % LSE_ROWS
    back = jnp.concatenate(
        [
            part.astype(jnp.bfloat16),
            lse_parts,
            jnp.zeros((sources, pad, width), jnp.bfloat16),
        ],
        axis=1,
    )
    got_back = lax.all_to_all(back, "ctx", split_axis=0, concat_axis=0, tiled=True)
    rows_part = CAP * heads_loc * tile_rows
    got_out = got_back[:, :rows_part].reshape(sources, CAP, heads_loc, tile_rows, width)
    got_lse = join_bf16(
        jnp.transpose(
            got_back[:, rows_part : rows_part + lse_parts.shape[1]].reshape(sources, 3, rows_part),
            (1, 0, 2),
        )
    ).reshape(sources, CAP, heads_loc, tile_rows)

    clipped = jnp.clip(target, 0, sources - 1)
    pick_out = got_out[clipped, slot, head_idx].astype(jnp.float32)
    pick_lse = got_lse[clipped, slot, head_idx]
    keep = valid[..., None]
    top = jnp.maximum(own_lse, jnp.max(jnp.where(keep, pick_lse, own_lse[:, :, None]), axis=2))
    own_w = jnp.exp(own_lse - top)
    pick_w = jnp.exp(jnp.where(keep, pick_lse - top[:, :, None], jnp.float32(-1e30)))
    numer = own_w[..., None] * own_out + jnp.sum(pick_w[..., None] * pick_out, axis=2)
    denom = own_w + jnp.sum(pick_w, axis=2)
    attention = jnp.transpose(numer / denom[..., None], (1, 2, 0, 3)).reshape(
        tokens_here, heads_loc * width
    )
    attention = attention.astype(jnp.bfloat16)
    gathered = lax.all_gather(attention, ("y", "zh"), axis=1, tiled=True)
    projected = jnp.dot(
        gathered,
        out_weight,
        preferred_element_type=jnp.float32,
    )
    return projected.astype(jnp.bfloat16)


def solution(mesh):
    ctx_n, head_n = mesh.devices.shape
    split = Mesh(mesh.devices.reshape(ctx_n, head_n // 2, 2), ("ctx", "y", "zh"))
    head = ("y", "zh")
    return jax.shard_map(
        local,
        mesh=split,
        in_specs=(
            P("ctx", head),
            P("ctx", head),
            P("ctx", head),
            P(head, "ctx", None),
            P(None, head),
        ),
        out_specs=P("ctx", head),
        check_vma=False,
    )
```

```python
import jax
import jax.numpy as jnp
from jax import lax
from jax.sharding import Mesh, PartitionSpec as P

CAP = 2


def split_bf16(x):
    hi = lax.reduce_precision(x, exponent_bits=8, mantissa_bits=7)
    rest = x - hi
    mid = lax.reduce_precision(rest, exponent_bits=8, mantissa_bits=7)
    lo = rest - mid
    return jnp.stack([hi, mid, lo]).astype(jnp.bfloat16)


def join_bf16(parts):
    parts = parts.astype(jnp.float32)
    return parts[0] + (parts[1] + parts[2])


def softmax_pv(scores, vals):
    top = jnp.max(scores, axis=-1)
    prob = jnp.exp(scores - top[..., None])
    total = jnp.sum(prob, axis=-1)
    part = jnp.einsum(
        "hrk,khd->hrd", prob.astype(jnp.bfloat16), vals, preferred_element_type=jnp.float32
    )
    return part / total[..., None], top + jnp.log(total)


def local(queries, keys, values, selected, out_weight):
    heads_loc = selected.shape[0]
    tiles = selected.shape[1]
    tokens_here = queries.shape[0]
    width = queries.shape[1] // heads_loc
    tile_rows = tokens_here // tiles
    sources = lax.axis_size("ctx")
    mine = lax.axis_index("ctx")
    scale = width ** (-0.5)
    quer_three = queries.reshape(tokens_here, heads_loc, width)
    keys_three = keys.reshape(tokens_here, heads_loc, width)
    vals_three = values.reshape(tokens_here, heads_loc, width)

    pos = jnp.arange(tokens_here, dtype=jnp.int32)
    own_scores = (
        jnp.einsum("rhd,khd->hrk", quer_three, keys_three, preferred_element_type=jnp.float32)
        * scale
    )
    own_scores = jnp.where((pos[:, None] >= pos[None, :])[None], own_scores, jnp.float32(-1e30))
    own_out, own_lse = softmax_pv(own_scores, vals_three)
    own_out = own_out.reshape(heads_loc, tiles, tile_rows, width)
    own_lse = own_lse.reshape(heads_loc, tiles, tile_rows)

    picks = selected[:, :, 1:]
    valid = picks != mine
    target = jnp.where(valid, picks, sources)
    onehot = (target[..., None] == jnp.arange(sources, dtype=jnp.int32)).astype(jnp.int32)
    flat_hot = onehot.reshape(heads_loc, tiles * 2, sources)
    before = jnp.cumsum(flat_hot, axis=1) - flat_hot
    slot = jnp.sum(before * flat_hot, axis=-1).reshape(heads_loc, tiles, 2)
    query_src = jnp.transpose(
        quer_three.reshape(tiles, tile_rows, heads_loc, width), (2, 0, 1, 3)
    ).reshape(heads_loc, tiles, tile_rows * width)
    flat_slot = target * CAP + slot
    route = (
        flat_slot[..., None] == jnp.arange(sources * CAP, dtype=jnp.int32)
    ).astype(jnp.bfloat16)
    send_q = jnp.einsum(
        "htep,htx->phx", route, query_src, preferred_element_type=jnp.float32
    ).astype(jnp.bfloat16)
    send_q = send_q.reshape(sources, CAP, heads_loc, tile_rows, width)
    got_rows = lax.all_to_all(send_q, "ctx", split_axis=0, concat_axis=0, tiled=True)

    got_q = jnp.transpose(got_rows, (2, 0, 1, 3, 4)).reshape(
        heads_loc, sources * CAP * tile_rows, width
    )
    got_scores = (
        jnp.einsum("hrd,khd->hrk", got_q, keys_three, preferred_element_type=jnp.float32) * scale
    )
    part, lse = softmax_pv(got_scores, vals_three)
    part = jnp.transpose(
        part.reshape(heads_loc, sources, CAP, tile_rows, width), (1, 2, 0, 3, 4)
    ).reshape(sources, CAP * heads_loc * tile_rows, width)
    lse = jnp.transpose(lse.reshape(heads_loc, sources, CAP, tile_rows), (1, 2, 0, 3)).reshape(
        sources, CAP * heads_loc * tile_rows
    )
    lse_parts = jnp.transpose(split_bf16(lse), (1, 0, 2))
    rows_part = CAP * heads_loc * tile_rows
    back = jnp.concatenate(
        [
            part.astype(jnp.bfloat16).reshape(sources, rows_part * width),
            lse_parts.reshape(sources, 3 * rows_part),
        ],
        axis=1,
    )
    got_back = lax.all_to_all(back, "ctx", split_axis=0, concat_axis=0, tiled=True)
    got_out = got_back[:, : rows_part * width].reshape(sources * CAP, heads_loc, tile_rows * width)
    got_parts = jnp.transpose(
        got_back[:, rows_part * width :].reshape(sources, 3, CAP, heads_loc, tile_rows),
        (0, 2, 3, 1, 4),
    ).reshape(sources * CAP, heads_loc, 3 * tile_rows)
    pick_out = jnp.einsum(
        "htep,phx->htex", route, got_out, preferred_element_type=jnp.float32
    ).reshape(heads_loc, tiles, 2, tile_rows, width)
    pick_parts = jnp.einsum(
        "htep,phx->htex", route, got_parts, preferred_element_type=jnp.float32
    ).reshape(heads_loc, tiles, 2, 3, tile_rows)
    pick_lse = pick_parts[:, :, :, 0] + (pick_parts[:, :, :, 1] + pick_parts[:, :, :, 2])
    keep = valid[..., None]
    top = jnp.maximum(own_lse, jnp.max(jnp.where(keep, pick_lse, own_lse[:, :, None]), axis=2))
    own_w = jnp.exp(own_lse - top)
    pick_w = jnp.exp(jnp.where(keep, pick_lse - top[:, :, None], jnp.float32(-1e30)))
    numer = own_w[..., None] * own_out + jnp.sum(pick_w[..., None] * pick_out, axis=2)
    denom = own_w + jnp.sum(pick_w, axis=2)
    attention = jnp.transpose(numer / denom[..., None], (1, 2, 0, 3)).reshape(
        tokens_here, heads_loc * width
    )
    attention = attention.astype(jnp.bfloat16)
    gathered = lax.all_gather(attention, "zh", axis=1, tiled=True)
    gathered = lax.all_gather(gathered, "y", axis=1, tiled=True)
    projected = jnp.dot(
        gathered,
        out_weight,
        preferred_element_type=jnp.float32,
    )
    return projected.astype(jnp.bfloat16)


def solution(mesh):
    ctx_n, head_n = mesh.devices.shape
    split = Mesh(mesh.devices.reshape(ctx_n, head_n // 2, 2), ("ctx", "y", "zh"))
    head = ("y", "zh")
    return jax.shard_map(
        local,
        mesh=split,
        in_specs=(
            P("ctx", head),
            P("ctx", head),
            P("ctx", head),
            P(head, "ctx", None),
            P(None, head),
        ),
        out_specs=P("ctx", head),
        check_vma=False,
    )
```

```python
import jax
import jax.numpy as jnp
from jax import lax
from jax.sharding import Mesh, PartitionSpec as P

CAP = 2
LSE_ROWS = 16


def split_bf16(x):
    hi = lax.reduce_precision(x, exponent_bits=8, mantissa_bits=7)
    rest = x - hi
    mid = lax.reduce_precision(rest, exponent_bits=8, mantissa_bits=7)
    lo = rest - mid
    return jnp.stack([hi, mid, lo]).astype(jnp.bfloat16)


def join_bf16(parts):
    parts = parts.astype(jnp.float32)
    return parts[0] + (parts[1] + parts[2])


def softmax_pv(scores, vals):
    top = jnp.max(scores, axis=-1)
    prob = jnp.exp(scores - top[..., None])
    total = jnp.sum(prob, axis=-1)
    part = jnp.einsum(
        "hrk,khd->hrd", prob.astype(jnp.bfloat16), vals, preferred_element_type=jnp.float32
    )
    return part / total[..., None], top + jnp.log(total)


def local(queries, keys, values, selected, out_weight):
    heads_loc = selected.shape[0]
    tiles = selected.shape[1]
    tokens_here = queries.shape[0]
    width = queries.shape[1] // heads_loc
    tile_rows = tokens_here // tiles
    sources = lax.axis_size("ctx")
    mine = lax.axis_index("ctx")
    scale = width ** (-0.5)
    quer_three = queries.reshape(tokens_here, heads_loc, width)
    keys_three = keys.reshape(tokens_here, heads_loc, width)
    vals_three = values.reshape(tokens_here, heads_loc, width)

    pos = jnp.arange(tokens_here, dtype=jnp.int32)
    own_scores = (
        jnp.einsum("rhd,khd->hrk", quer_three, keys_three, preferred_element_type=jnp.float32)
        * scale
    )
    own_scores = jnp.where((pos[:, None] >= pos[None, :])[None], own_scores, jnp.float32(-1e30))
    own_out, own_lse = softmax_pv(own_scores, vals_three)
    own_out = own_out.reshape(heads_loc, tiles, tile_rows, width)
    own_lse = own_lse.reshape(heads_loc, tiles, tile_rows)

    picks = selected[:, :, 1:]
    valid = picks != mine
    target = jnp.where(valid, picks, sources)
    onehot = (target[..., None] == jnp.arange(sources, dtype=jnp.int32)).astype(jnp.int32)
    flat_hot = onehot.reshape(heads_loc, tiles * 2, sources)
    before = jnp.cumsum(flat_hot, axis=1) - flat_hot
    slot = jnp.sum(before * flat_hot, axis=-1).reshape(heads_loc, tiles, 2)
    query_src = jnp.transpose(
        quer_three.reshape(tiles, tile_rows, heads_loc, width), (2, 0, 1, 3)
    ).reshape(heads_loc, tiles, tile_rows * width)
    flat_slot = target * CAP + slot
    route = (
        flat_slot[..., None] == jnp.arange(sources * CAP, dtype=jnp.int32)
    ).astype(jnp.bfloat16)
    send_q = jnp.einsum(
        "htep,htx->phx", route, query_src, preferred_element_type=jnp.float32
    ).astype(jnp.bfloat16)
    send_q = send_q.reshape(sources, CAP, heads_loc, tile_rows, width)
    got_rows = lax.all_to_all(send_q, "ctx", split_axis=0, concat_axis=0, tiled=True)

    got_q = jnp.transpose(got_rows, (2, 0, 1, 3, 4)).reshape(
        heads_loc, sources * CAP * tile_rows, width
    )
    got_scores = (
        jnp.einsum("hrd,khd->hrk", got_q, keys_three, preferred_element_type=jnp.float32) * scale
    )
    part, lse = softmax_pv(got_scores, vals_three)
    part = jnp.transpose(
        part.reshape(heads_loc, sources, CAP, tile_rows, width), (1, 2, 0, 3, 4)
    ).reshape(sources, CAP * heads_loc * tile_rows, width)
    lse = jnp.transpose(lse.reshape(heads_loc, sources, CAP, tile_rows), (1, 2, 0, 3)).reshape(
        sources, CAP * heads_loc * tile_rows
    )
    lse_parts = jnp.transpose(split_bf16(lse), (1, 0, 2)).reshape(sources, -1, width)
    pad = -lse_parts.shape[1] % LSE_ROWS
    back = jnp.concatenate(
        [
            part.astype(jnp.bfloat16),
            lse_parts,
            jnp.zeros((sources, pad, width), jnp.bfloat16),
        ],
        axis=1,
    )
    got_back = lax.all_to_all(back, "ctx", split_axis=0, concat_axis=0, tiled=True)
    rows_part = CAP * heads_loc * tile_rows
    got_out = got_back[:, :rows_part].reshape(sources * CAP, heads_loc, tile_rows, width)
    got_parts = jnp.transpose(
        got_back[:, rows_part : rows_part + lse_parts.shape[1]].reshape(
            sources, 3, CAP, heads_loc, tile_rows
        ),
        (0, 2, 3, 1, 4),
    ).reshape(sources * CAP, heads_loc, 3, tile_rows)
    pick_out = jnp.einsum(
        "htep,phrd->hterd", route, got_out, preferred_element_type=jnp.float32
    )
    pick_parts = jnp.einsum(
        "htep,phkr->htekr", route, got_parts, preferred_element_type=jnp.float32
    )
    pick_lse = pick_parts[:, :, :, 0] + (pick_parts[:, :, :, 1] + pick_parts[:, :, :, 2])
    keep = valid[..., None]
    top = jnp.maximum(own_lse, jnp.max(jnp.where(keep, pick_lse, own_lse[:, :, None]), axis=2))
    own_w = jnp.exp(own_lse - top)
    pick_w = jnp.exp(jnp.where(keep, pick_lse - top[:, :, None], jnp.float32(-1e30)))
    numer = own_w[..., None] * own_out + jnp.sum(pick_w[..., None] * pick_out, axis=2)
    denom = own_w + jnp.sum(pick_w, axis=2)
    attention = jnp.transpose(numer / denom[..., None], (1, 2, 0, 3)).reshape(
        tokens_here, heads_loc * width
    )
    attention = attention.astype(jnp.bfloat16)
    gathered = lax.all_gather(attention, "zh", axis=1, tiled=True)
    gathered = lax.all_gather(gathered, "y", axis=1, tiled=True)
    projected = jnp.dot(
        gathered,
        out_weight,
        preferred_element_type=jnp.float32,
    )
    return projected.astype(jnp.bfloat16)


def solution(mesh):
    ctx_n, head_n = mesh.devices.shape
    split = Mesh(mesh.devices.reshape(ctx_n, head_n // 2, 2), ("ctx", "y", "zh"))
    head = ("y", "zh")
    return jax.shard_map(
        local,
        mesh=split,
        in_specs=(
            P("ctx", head),
            P("ctx", head),
            P("ctx", head),
            P(head, "ctx", None),
            P(None, head),
        ),
        out_specs=P("ctx", head),
        check_vma=False,
    )
```

```python
import jax
import jax.numpy as jnp
from jax import lax
from jax.sharding import Mesh, PartitionSpec as P

CAP = 2
LSE_ROWS = 16


def split_bf16(x):
    hi = lax.reduce_precision(x, exponent_bits=8, mantissa_bits=7)
    rest = x - hi
    mid = lax.reduce_precision(rest, exponent_bits=8, mantissa_bits=7)
    lo = rest - mid
    return jnp.stack([hi, mid, lo]).astype(jnp.bfloat16)


def join_bf16(parts):
    parts = parts.astype(jnp.float32)
    return parts[0] + (parts[1] + parts[2])


def softmax_pv(scores, vals):
    top = jnp.max(scores, axis=-1)
    prob = jnp.exp(scores - top[..., None])
    total = jnp.sum(prob, axis=-1)
    part = jnp.einsum(
        "hrk,khd->hrd", prob.astype(jnp.bfloat16), vals, preferred_element_type=jnp.float32
    )
    return part / total[..., None], top + jnp.log(total)


def local(queries, keys, values, selected, out_weight):
    heads_loc = selected.shape[0]
    tiles = selected.shape[1]
    tokens_here = queries.shape[0]
    width = queries.shape[1] // heads_loc
    tile_rows = tokens_here // tiles
    sources = lax.axis_size("ctx")
    mine = lax.axis_index("ctx")
    scale = width ** (-0.5)
    quer_three = queries.reshape(tokens_here, heads_loc, width)
    keys_three = keys.reshape(tokens_here, heads_loc, width)
    vals_three = values.reshape(tokens_here, heads_loc, width)

    pos = jnp.arange(tokens_here, dtype=jnp.int32)
    own_scores = (
        jnp.einsum("rhd,khd->hrk", quer_three, keys_three, preferred_element_type=jnp.float32)
        * scale
    )
    own_scores = jnp.where((pos[:, None] >= pos[None, :])[None], own_scores, jnp.float32(-1e30))
    own_out, own_lse = softmax_pv(own_scores, vals_three)
    own_out = own_out.reshape(heads_loc, tiles, tile_rows, width)
    own_lse = own_lse.reshape(heads_loc, tiles, tile_rows)

    picks = selected[:, :, 1:]
    valid = picks != mine
    target = jnp.where(valid, picks, sources)
    onehot = (target[..., None] == jnp.arange(sources, dtype=jnp.int32)).astype(jnp.int32)
    flat_hot = onehot.reshape(heads_loc, tiles * 2, sources)
    before = jnp.cumsum(flat_hot, axis=1) - flat_hot
    slot = jnp.sum(before * flat_hot, axis=-1).reshape(heads_loc, tiles, 2)
    query_src = jnp.transpose(
        quer_three.reshape(tiles, tile_rows, heads_loc, width), (2, 0, 1, 3)
    ).reshape(heads_loc, tiles, tile_rows * width)
    flat_slot = target * CAP + slot
    route = (
        flat_slot[..., None] == jnp.arange(sources * CAP, dtype=jnp.int32)
    ).astype(jnp.bfloat16)
    send_q = jnp.einsum(
        "htep,htx->phx", route, query_src, preferred_element_type=jnp.float32
    ).astype(jnp.bfloat16)
    send_q = send_q.reshape(sources, CAP, heads_loc, tile_rows, width)
    got_rows = lax.all_to_all(send_q, "ctx", split_axis=0, concat_axis=0, tiled=True)

    got_q = jnp.transpose(got_rows, (2, 0, 1, 3, 4)).reshape(
        heads_loc, sources * CAP * tile_rows, width
    )
    got_scores = (
        jnp.einsum("hrd,khd->hrk", got_q, keys_three, preferred_element_type=jnp.float32) * scale
    )
    part, lse = softmax_pv(got_scores, vals_three)
    part = jnp.transpose(
        part.reshape(heads_loc, sources, CAP, tile_rows, width), (1, 2, 0, 3, 4)
    ).reshape(sources, CAP * heads_loc * tile_rows, width)
    lse = jnp.transpose(lse.reshape(heads_loc, sources, CAP, tile_rows), (1, 2, 0, 3)).reshape(
        sources, CAP * heads_loc * tile_rows
    )
    lse_parts = jnp.transpose(split_bf16(lse), (1, 0, 2)).reshape(sources, -1, width)
    pad = -lse_parts.shape[1] % LSE_ROWS
    back = jnp.concatenate(
        [
            part.astype(jnp.bfloat16),
            lse_parts,
            jnp.zeros((sources, pad, width), jnp.bfloat16),
        ],
        axis=1,
    )
    got_back = lax.all_to_all(back, "ctx", split_axis=0, concat_axis=0, tiled=True)
    rows_part = CAP * heads_loc * tile_rows
    got_out = got_back[:, :rows_part].reshape(sources * CAP, heads_loc, tile_rows, width)
    got_parts = jnp.transpose(
        got_back[:, rows_part : rows_part + lse_parts.shape[1]].reshape(
            sources, 3, CAP, heads_loc, tile_rows
        ),
        (0, 2, 3, 1, 4),
    ).reshape(sources * CAP, heads_loc, 3, tile_rows)
    pick_out = jnp.einsum(
        "htep,phrd->hterd", route, got_out, preferred_element_type=jnp.float32
    )
    pick_parts = jnp.einsum(
        "htep,phkr->htekr", route, got_parts, preferred_element_type=jnp.float32
    )
    pick_lse = pick_parts[:, :, :, 0] + (pick_parts[:, :, :, 1] + pick_parts[:, :, :, 2])
    keep = valid[..., None]
    top = jnp.maximum(own_lse, jnp.max(jnp.where(keep, pick_lse, own_lse[:, :, None]), axis=2))
    own_w = jnp.exp(own_lse - top)
    pick_w = jnp.exp(jnp.where(keep, pick_lse - top[:, :, None], jnp.float32(-1e30)))
    numer = own_w[..., None] * own_out + jnp.sum(pick_w[..., None] * pick_out, axis=2)
    denom = own_w + jnp.sum(pick_w, axis=2)
    attention = jnp.transpose(numer / denom[..., None], (1, 2, 0, 3)).reshape(
        tokens_here, heads_loc * width
    )
    attention = attention.astype(jnp.bfloat16)
    pair = lax.axis_size("zh")
    mine_zh = lax.axis_index("zh")
    own_rows = lax.all_gather(attention, "y", axis=1, tiled=True)
    partner = lax.ppermute(attention, "zh", [(0, 1), (1, 0)])
    partner_rows = lax.all_gather(partner, "y", axis=1, tiled=True)
    groups = out_weight.reshape(-1, pair, heads_loc * width, out_weight.shape[1])
    own_w = lax.dynamic_index_in_dim(groups, mine_zh, axis=1, keepdims=False)
    partner_w = lax.dynamic_index_in_dim(groups, 1 - mine_zh, axis=1, keepdims=False)
    projected = jnp.dot(
        own_rows, own_w.reshape(-1, out_weight.shape[1]), preferred_element_type=jnp.float32
    ) + jnp.dot(
        partner_rows, partner_w.reshape(-1, out_weight.shape[1]), preferred_element_type=jnp.float32
    )
    return projected.astype(jnp.bfloat16)


def solution(mesh):
    ctx_n, head_n = mesh.devices.shape
    split = Mesh(mesh.devices.reshape(ctx_n, head_n // 2, 2), ("ctx", "y", "zh"))
    head = ("y", "zh")
    return jax.shard_map(
        local,
        mesh=split,
        in_specs=(
            P("ctx", head),
            P("ctx", head),
            P("ctx", head),
            P(head, "ctx", None),
            P(None, head),
        ),
        out_specs=P("ctx", head),
        check_vma=False,
    )
```

```python
import jax
import jax.numpy as jnp
from jax import lax
from jax.sharding import Mesh, PartitionSpec as P

CAP = 2
LANE_ROWS = 4
LSE_ROWS = 16


def split_bf16(x):
    hi = lax.reduce_precision(x, exponent_bits=8, mantissa_bits=7)
    rest = x - hi
    mid = lax.reduce_precision(rest, exponent_bits=8, mantissa_bits=7)
    lo = rest - mid
    return jnp.stack([hi, mid, lo]).astype(jnp.bfloat16)


def join_bf16(parts):
    parts = parts.astype(jnp.float32)
    return parts[0] + (parts[1] + parts[2])


def softmax_pv(scores, vals):
    top = jnp.max(scores, axis=-1)
    prob = jnp.exp(scores - top[..., None])
    total = jnp.sum(prob, axis=-1)
    part = jnp.einsum(
        "hrk,khd->hrd", prob.astype(jnp.bfloat16), vals, preferred_element_type=jnp.float32
    )
    return part / total[..., None], top + jnp.log(total)


def local(queries, keys, values, selected, out_weight):
    heads_loc = selected.shape[0]
    tiles = selected.shape[1]
    tokens_here = queries.shape[0]
    width = queries.shape[1] // heads_loc
    tile_rows = tokens_here // tiles
    sources = lax.axis_size("ctx")
    mine = lax.axis_index("ctx")
    scale = width ** (-0.5)
    quer_three = queries.reshape(tokens_here, heads_loc, width)
    keys_three = keys.reshape(tokens_here, heads_loc, width)
    vals_three = values.reshape(tokens_here, heads_loc, width)

    pos = jnp.arange(tokens_here, dtype=jnp.int32)
    own_scores = (
        jnp.einsum("rhd,khd->hrk", quer_three, keys_three, preferred_element_type=jnp.float32)
        * scale
    )
    own_scores = jnp.where((pos[:, None] >= pos[None, :])[None], own_scores, jnp.float32(-1e30))
    own_out, own_lse = softmax_pv(own_scores, vals_three)
    own_out = own_out.reshape(heads_loc, tiles, tile_rows, width)
    own_lse = own_lse.reshape(heads_loc, tiles, tile_rows)

    picks = selected[:, :, 1:]
    valid = picks != mine
    target = jnp.where(valid, picks, sources)
    onehot = (target[..., None] == jnp.arange(sources, dtype=jnp.int32)).astype(jnp.int32)
    flat_hot = onehot.reshape(heads_loc, tiles * 2, sources)
    before = jnp.cumsum(flat_hot, axis=1) - flat_hot
    slot = jnp.sum(before * flat_hot, axis=-1).reshape(heads_loc, tiles, 2)
    query_src = jnp.transpose(
        quer_three.reshape(tiles, tile_rows, heads_loc, width), (2, 0, 1, 3)
    ).reshape(heads_loc, tiles, tile_rows * width)
    flat_slot = target * CAP + slot
    route = (
        flat_slot[..., None] == jnp.arange(sources * CAP, dtype=jnp.int32)
    ).astype(jnp.bfloat16)
    send_q = jnp.einsum(
        "htep,htx->phx", route, query_src, preferred_element_type=jnp.float32
    ).astype(jnp.bfloat16)
    send_q = send_q.reshape(sources, CAP, heads_loc, tile_rows, width)
    got_rows = lax.all_to_all(send_q, "ctx", split_axis=0, concat_axis=0, tiled=True)

    got_q = jnp.transpose(got_rows, (2, 0, 1, 3, 4)).reshape(
        heads_loc, sources * CAP * tile_rows, width
    )
    got_scores = (
        jnp.einsum("hrd,khd->hrk", got_q, keys_three, preferred_element_type=jnp.float32) * scale
    )
    part, lse = softmax_pv(got_scores, vals_three)
    part = jnp.transpose(
        part.reshape(heads_loc, sources, CAP, tile_rows, width), (1, 2, 0, 3, 4)
    ).reshape(sources, CAP * heads_loc * tile_rows, width)
    pieces = split_bf16(lse.reshape(heads_loc, sources, CAP, tile_rows))
    pieces = jnp.concatenate(
        [pieces, jnp.zeros((LANE_ROWS - 3,) + pieces.shape[1:], pieces.dtype)], axis=0
    )
    lse_rows = jnp.transpose(pieces, (2, 3, 1, 0, 4)).reshape(
        sources, CAP * heads_loc, LANE_ROWS * tile_rows
    )
    rows_part = CAP * heads_loc * tile_rows
    pad = -(rows_part + CAP * heads_loc) % 16
    back = jnp.concatenate(
        [
            part.astype(jnp.bfloat16),
            lse_rows,
            jnp.zeros((sources, pad, width), jnp.bfloat16),
        ],
        axis=1,
    )
    got_back = lax.all_to_all(back, "ctx", split_axis=0, concat_axis=0, tiled=True)
    got_out = got_back[:, :rows_part].reshape(sources * CAP, heads_loc, tile_rows, width)
    got_lse = got_back[:, rows_part : rows_part + CAP * heads_loc].reshape(
        sources * CAP, heads_loc, width
    )
    pick_out = jnp.einsum(
        "htep,phrd->hterd", route, got_out, preferred_element_type=jnp.float32
    )
    pick_parts = jnp.einsum(
        "htep,phx->htex", route, got_lse, preferred_element_type=jnp.float32
    ).reshape(heads_loc, tiles, 2, LANE_ROWS, tile_rows)
    pick_lse = pick_parts[:, :, :, 0] + (pick_parts[:, :, :, 1] + pick_parts[:, :, :, 2])
    keep = valid[..., None]
    top = jnp.maximum(own_lse, jnp.max(jnp.where(keep, pick_lse, own_lse[:, :, None]), axis=2))
    own_w = jnp.exp(own_lse - top)
    pick_w = jnp.exp(jnp.where(keep, pick_lse - top[:, :, None], jnp.float32(-1e30)))
    numer = own_w[..., None] * own_out + jnp.sum(pick_w[..., None] * pick_out, axis=2)
    denom = own_w + jnp.sum(pick_w, axis=2)
    attention = jnp.transpose(numer / denom[..., None], (1, 2, 0, 3)).reshape(
        tokens_here, heads_loc * width
    )
    attention = attention.astype(jnp.bfloat16)
    pair = lax.axis_size("zh")
    mine_zh = lax.axis_index("zh")
    own_rows = lax.all_gather(attention, "y", axis=1, tiled=True)
    partner = lax.ppermute(attention, "zh", [(0, 1), (1, 0)])
    partner_rows = lax.all_gather(partner, "y", axis=1, tiled=True)
    groups = out_weight.reshape(-1, pair, heads_loc * width, out_weight.shape[1])
    own_w = lax.dynamic_index_in_dim(groups, mine_zh, axis=1, keepdims=False)
    partner_w = lax.dynamic_index_in_dim(groups, 1 - mine_zh, axis=1, keepdims=False)
    projected = jnp.dot(
        own_rows, own_w.reshape(-1, out_weight.shape[1]), preferred_element_type=jnp.float32
    ) + jnp.dot(
        partner_rows, partner_w.reshape(-1, out_weight.shape[1]), preferred_element_type=jnp.float32
    )
    return projected.astype(jnp.bfloat16)


def solution(mesh):
    ctx_n, head_n = mesh.devices.shape
    split = Mesh(mesh.devices.reshape(ctx_n, head_n // 2, 2), ("ctx", "y", "zh"))
    head = ("y", "zh")
    return jax.shard_map(
        local,
        mesh=split,
        in_specs=(
            P("ctx", head),
            P("ctx", head),
            P("ctx", head),
            P(head, "ctx", None),
            P(None, head),
        ),
        out_specs=P("ctx", head),
        check_vma=False,
    )
```

```python
import functools

import jax
import jax.numpy as jnp
from jax import lax
from jax.experimental import pallas as pl
from jax.experimental.pallas import tpu as pltpu
from jax.sharding import Mesh, PartitionSpec as P

CAP = 2
LANE_ROWS = 4
LSE_ROWS = 16


def split_bf16(x):
    hi = lax.reduce_precision(x, exponent_bits=8, mantissa_bits=7)
    rest = x - hi
    mid = lax.reduce_precision(rest, exponent_bits=8, mantissa_bits=7)
    lo = rest - mid
    return jnp.stack([hi, mid, lo]).astype(jnp.bfloat16)


def join_bf16(parts):
    parts = parts.astype(jnp.float32)
    return parts[0] + (parts[1] + parts[2])


def softmax_pv(scores, vals):
    top = jnp.max(scores, axis=-1)
    prob = jnp.exp(scores - top[..., None])
    total = jnp.sum(prob, axis=-1)
    part = jnp.einsum(
        "hrk,khd->hrd", prob.astype(jnp.bfloat16), vals, preferred_element_type=jnp.float32
    )
    return part / total[..., None], top + jnp.log(total)


def owner_kernel(scale, q_ref, k_ref, v_ref, part_ref, lse_ref):
    groups = q_ref.shape[0]
    slots = q_ref.shape[1]
    rows = q_ref.shape[2]
    width = q_ref.shape[3]
    heads = k_ref.shape[1] // width
    nt = (((1,), (1,)), ((), ()))
    for j in range(slots):
        cols = pl.ds((j % heads) * width, width)
        q = q_ref[:, j].reshape(groups * rows, width)
        k = k_ref[:, cols]
        v = v_ref[:, cols]
        s = lax.dot_general(q, k, nt, preferred_element_type=jnp.float32) * scale
        top = jnp.max(s, axis=1, keepdims=True)
        prob = jnp.exp(s - top)
        total = jnp.sum(prob, axis=1, keepdims=True)
        out = jnp.dot(prob.astype(jnp.bfloat16), v, preferred_element_type=jnp.float32) / total
        part_ref[:, j] = out.reshape(groups, rows, width).astype(part_ref.dtype)
        s_t = lax.dot_general(k, q, nt, preferred_element_type=jnp.float32) * scale
        top_t = jnp.max(s_t, axis=0, keepdims=True)
        total_t = jnp.sum(jnp.exp(s_t - top_t), axis=0, keepdims=True)
        lse_ref[pl.ds(j, 1), :] = top_t + jnp.log(total_t)


def owner_attention(got, keys, values, scale):
    sources, slots, rows, width = got.shape
    step = 8
    return pl.pallas_call(
        functools.partial(owner_kernel, scale),
        grid=(sources // step,),
        in_specs=[
            pl.BlockSpec((step, slots, rows, width), lambda i: (i, 0, 0, 0)),
            pl.BlockSpec(keys.shape, lambda i: (0, 0)),
            pl.BlockSpec(values.shape, lambda i: (0, 0)),
        ],
        out_specs=[
            pl.BlockSpec((step, slots, rows, width), lambda i: (i, 0, 0, 0)),
            pl.BlockSpec((slots, step * rows), lambda i: (0, i)),
        ],
        out_shape=[
            jax.ShapeDtypeStruct(got.shape, jnp.bfloat16),
            jax.ShapeDtypeStruct((slots, sources * rows), jnp.float32),
        ],
        cost_estimate=pl.CostEstimate(
            flops=6 * sources * slots * rows * keys.shape[0] * width,
            transcendentals=2 * sources * slots * rows * keys.shape[0],
            bytes_accessed=2 * got.size * 2 + 4 * slots * sources * rows,
        ),
    )(got, keys, values)


def local(queries, keys, values, selected, out_weight):
    heads_loc = selected.shape[0]
    tiles = selected.shape[1]
    tokens_here = queries.shape[0]
    width = queries.shape[1] // heads_loc
    tile_rows = tokens_here // tiles
    sources = lax.axis_size("ctx")
    mine = lax.axis_index("ctx")
    scale = width ** (-0.5)
    quer_three = queries.reshape(tokens_here, heads_loc, width)
    keys_three = keys.reshape(tokens_here, heads_loc, width)
    vals_three = values.reshape(tokens_here, heads_loc, width)

    pos = jnp.arange(tokens_here, dtype=jnp.int32)
    own_scores = (
        jnp.einsum("rhd,khd->hrk", quer_three, keys_three, preferred_element_type=jnp.float32)
        * scale
    )
    own_scores = jnp.where((pos[:, None] >= pos[None, :])[None], own_scores, jnp.float32(-1e30))
    own_out, own_lse = softmax_pv(own_scores, vals_three)
    own_out = own_out.reshape(heads_loc, tiles, tile_rows, width)
    own_lse = own_lse.reshape(heads_loc, tiles, tile_rows)

    picks = selected[:, :, 1:]
    valid = picks != mine
    target = jnp.where(valid, picks, sources)
    onehot = (target[..., None] == jnp.arange(sources, dtype=jnp.int32)).astype(jnp.int32)
    flat_hot = onehot.reshape(heads_loc, tiles * 2, sources)
    before = jnp.cumsum(flat_hot, axis=1) - flat_hot
    slot = jnp.sum(before * flat_hot, axis=-1).reshape(heads_loc, tiles, 2)
    query_src = jnp.transpose(
        quer_three.reshape(tiles, tile_rows, heads_loc, width), (2, 0, 1, 3)
    ).reshape(heads_loc, tiles, tile_rows * width)
    flat_slot = target * CAP + slot
    route = (
        flat_slot[..., None] == jnp.arange(sources * CAP, dtype=jnp.int32)
    ).astype(jnp.bfloat16)
    send_q = jnp.einsum(
        "htep,htx->phx", route, query_src, preferred_element_type=jnp.float32
    ).astype(jnp.bfloat16)
    send_q = send_q.reshape(sources, CAP, heads_loc, tile_rows, width)
    got_rows = lax.all_to_all(send_q, "ctx", split_axis=0, concat_axis=0, tiled=True)

    part, lse = owner_attention(
        got_rows.reshape(sources, CAP * heads_loc, tile_rows, width), keys, values, scale
    )
    part = part.reshape(sources, CAP * heads_loc * tile_rows, width)
    pieces = split_bf16(lse.reshape(CAP, heads_loc, sources, tile_rows))
    pieces = jnp.concatenate(
        [pieces, jnp.zeros((LANE_ROWS - 3,) + pieces.shape[1:], pieces.dtype)], axis=0
    )
    lse_rows = jnp.transpose(pieces, (3, 1, 2, 0, 4)).reshape(
        sources, CAP * heads_loc, LANE_ROWS * tile_rows
    )
    rows_part = CAP * heads_loc * tile_rows
    pad = -(rows_part + CAP * heads_loc) % 16
    back = jnp.concatenate(
        [
            part.astype(jnp.bfloat16),
            lse_rows,
            jnp.zeros((sources, pad, width), jnp.bfloat16),
        ],
        axis=1,
    )
    got_back = lax.all_to_all(back, "ctx", split_axis=0, concat_axis=0, tiled=True)
    got_out = got_back[:, :rows_part].reshape(sources * CAP, heads_loc, tile_rows, width)
    got_lse = got_back[:, rows_part : rows_part + CAP * heads_loc].reshape(
        sources * CAP, heads_loc, width
    )
    pick_out = jnp.einsum(
        "htep,phrd->hterd", route, got_out, preferred_element_type=jnp.float32
    )
    pick_parts = jnp.einsum(
        "htep,phx->htex", route, got_lse, preferred_element_type=jnp.float32
    ).reshape(heads_loc, tiles, 2, LANE_ROWS, tile_rows)
    pick_lse = pick_parts[:, :, :, 0] + (pick_parts[:, :, :, 1] + pick_parts[:, :, :, 2])
    keep = valid[..., None]
    top = jnp.maximum(own_lse, jnp.max(jnp.where(keep, pick_lse, own_lse[:, :, None]), axis=2))
    own_w = jnp.exp(own_lse - top)
    pick_w = jnp.exp(jnp.where(keep, pick_lse - top[:, :, None], jnp.float32(-1e30)))
    numer = own_w[..., None] * own_out + jnp.sum(pick_w[..., None] * pick_out, axis=2)
    denom = own_w + jnp.sum(pick_w, axis=2)
    attention = jnp.transpose(numer / denom[..., None], (1, 2, 0, 3)).reshape(
        tokens_here, heads_loc * width
    )
    attention = attention.astype(jnp.bfloat16)
    pair = lax.axis_size("zh")
    mine_zh = lax.axis_index("zh")
    own_rows = lax.all_gather(attention, "y", axis=1, tiled=True)
    partner = lax.ppermute(attention, "zh", [(0, 1), (1, 0)])
    partner_rows = lax.all_gather(partner, "y", axis=1, tiled=True)
    groups = out_weight.reshape(-1, pair, heads_loc * width, out_weight.shape[1])
    own_w = lax.dynamic_index_in_dim(groups, mine_zh, axis=1, keepdims=False)
    partner_w = lax.dynamic_index_in_dim(groups, 1 - mine_zh, axis=1, keepdims=False)
    projected = jnp.dot(
        own_rows, own_w.reshape(-1, out_weight.shape[1]), preferred_element_type=jnp.float32
    ) + jnp.dot(
        partner_rows, partner_w.reshape(-1, out_weight.shape[1]), preferred_element_type=jnp.float32
    )
    return projected.astype(jnp.bfloat16)


def solution(mesh):
    ctx_n, head_n = mesh.devices.shape
    split = Mesh(mesh.devices.reshape(ctx_n, head_n // 2, 2), ("ctx", "y", "zh"))
    head = ("y", "zh")
    return jax.shard_map(
        local,
        mesh=split,
        in_specs=(
            P("ctx", head),
            P("ctx", head),
            P("ctx", head),
            P(head, "ctx", None),
            P(None, head),
        ),
        out_specs=P("ctx", head),
        check_vma=False,
    )
```

```python
import functools

import jax
import jax.numpy as jnp
from jax import lax
from jax.experimental import pallas as pl
from jax.experimental.pallas import tpu as pltpu
from jax.sharding import Mesh, PartitionSpec as P

CAP = 2
LANE_ROWS = 4
LSE_ROWS = 16


def split_bf16(x):
    hi = lax.reduce_precision(x, exponent_bits=8, mantissa_bits=7)
    rest = x - hi
    mid = lax.reduce_precision(rest, exponent_bits=8, mantissa_bits=7)
    lo = rest - mid
    return jnp.stack([hi, mid, lo]).astype(jnp.bfloat16)


def join_bf16(parts):
    parts = parts.astype(jnp.float32)
    return parts[0] + (parts[1] + parts[2])


def softmax_pv(scores, vals):
    top = jnp.max(scores, axis=-1)
    prob = jnp.exp(scores - top[..., None])
    total = jnp.sum(prob, axis=-1)
    part = jnp.einsum(
        "hrk,khd->hrd", prob.astype(jnp.bfloat16), vals, preferred_element_type=jnp.float32
    )
    return part / total[..., None], top + jnp.log(total)


def owner_kernel(scale, q_ref, k_ref, v_ref, part_ref, lse_ref):
    groups = q_ref.shape[0]
    slots = q_ref.shape[1]
    rows = q_ref.shape[2]
    width = q_ref.shape[3]
    heads = k_ref.shape[1] // width
    nt = (((1,), (1,)), ((), ()))
    tn = (((0,), (0,)), ((), ()))
    for j in range(slots):
        cols = pl.ds((j % heads) * width, width)
        q = q_ref[:, j].reshape(groups * rows, width)
        k = k_ref[:, cols]
        v = v_ref[:, cols]
        s_t = lax.dot_general(k, q, nt, preferred_element_type=jnp.float32) * scale
        top_t = jnp.max(s_t, axis=0, keepdims=True)
        prob_t = jnp.exp(s_t - top_t)
        total_t = jnp.sum(prob_t, axis=0, keepdims=True)
        out_t = lax.dot_general(
            v, prob_t.astype(jnp.bfloat16), tn, preferred_element_type=jnp.float32
        ) / total_t
        part_ref[:, j] = out_t.T.reshape(groups, rows, width).astype(part_ref.dtype)
        lse_ref[pl.ds(j, 1), :] = top_t + jnp.log(total_t)


def owner_attention(got, keys, values, scale):
    sources, slots, rows, width = got.shape
    step = 16
    return pl.pallas_call(
        functools.partial(owner_kernel, scale),
        grid=(sources // step,),
        in_specs=[
            pl.BlockSpec((step, slots, rows, width), lambda i: (i, 0, 0, 0)),
            pl.BlockSpec(keys.shape, lambda i: (0, 0)),
            pl.BlockSpec(values.shape, lambda i: (0, 0)),
        ],
        out_specs=[
            pl.BlockSpec((step, slots, rows, width), lambda i: (i, 0, 0, 0)),
            pl.BlockSpec((slots, step * rows), lambda i: (0, i)),
        ],
        out_shape=[
            jax.ShapeDtypeStruct(got.shape, jnp.bfloat16),
            jax.ShapeDtypeStruct((slots, sources * rows), jnp.float32),
        ],
        cost_estimate=pl.CostEstimate(
            flops=6 * sources * slots * rows * keys.shape[0] * width,
            transcendentals=2 * sources * slots * rows * keys.shape[0],
            bytes_accessed=2 * got.size * 2 + 4 * slots * sources * rows,
        ),
    )(got, keys, values)


def local(queries, keys, values, selected, out_weight):
    heads_loc = selected.shape[0]
    tiles = selected.shape[1]
    tokens_here = queries.shape[0]
    width = queries.shape[1] // heads_loc
    tile_rows = tokens_here // tiles
    sources = lax.axis_size("ctx")
    mine = lax.axis_index("ctx")
    scale = width ** (-0.5)
    quer_three = queries.reshape(tokens_here, heads_loc, width)
    keys_three = keys.reshape(tokens_here, heads_loc, width)
    vals_three = values.reshape(tokens_here, heads_loc, width)

    pos = jnp.arange(tokens_here, dtype=jnp.int32)
    own_scores = (
        jnp.einsum("rhd,khd->hrk", quer_three, keys_three, preferred_element_type=jnp.float32)
        * scale
    )
    own_scores = jnp.where((pos[:, None] >= pos[None, :])[None], own_scores, jnp.float32(-1e30))
    own_out, own_lse = softmax_pv(own_scores, vals_three)
    own_out = own_out.reshape(heads_loc, tiles, tile_rows, width)
    own_lse = own_lse.reshape(heads_loc, tiles, tile_rows)

    picks = selected[:, :, 1:]
    valid = picks != mine
    target = jnp.where(valid, picks, sources)
    onehot = (target[..., None] == jnp.arange(sources, dtype=jnp.int32)).astype(jnp.int32)
    flat_hot = onehot.reshape(heads_loc, tiles * 2, sources)
    before = jnp.cumsum(flat_hot, axis=1) - flat_hot
    slot = jnp.sum(before * flat_hot, axis=-1).reshape(heads_loc, tiles, 2)
    query_src = jnp.transpose(
        quer_three.reshape(tiles, tile_rows, heads_loc, width), (2, 0, 1, 3)
    ).reshape(heads_loc, tiles, tile_rows * width)
    flat_slot = target * CAP + slot
    route = (
        flat_slot[..., None] == jnp.arange(sources * CAP, dtype=jnp.int32)
    ).astype(jnp.bfloat16)
    send_q = jnp.einsum(
        "htep,htx->phx", route, query_src, preferred_element_type=jnp.float32
    ).astype(jnp.bfloat16)
    send_q = send_q.reshape(sources, CAP, heads_loc, tile_rows, width)
    got_rows = lax.all_to_all(send_q, "ctx", split_axis=0, concat_axis=0, tiled=True)

    part, lse = owner_attention(
        got_rows.reshape(sources, CAP * heads_loc, tile_rows, width), keys, values, scale
    )
    part = part.reshape(sources, CAP * heads_loc * tile_rows, width)
    pieces = split_bf16(lse.reshape(CAP, heads_loc, sources, tile_rows))
    pieces = jnp.concatenate(
        [pieces, jnp.zeros((LANE_ROWS - 3,) + pieces.shape[1:], pieces.dtype)], axis=0
    )
    lse_rows = jnp.transpose(pieces, (3, 1, 2, 0, 4)).reshape(
        sources, CAP * heads_loc, LANE_ROWS * tile_rows
    )
    rows_part = CAP * heads_loc * tile_rows
    pad = -(rows_part + CAP * heads_loc) % 16
    back = jnp.concatenate(
        [
            part.astype(jnp.bfloat16),
            lse_rows,
            jnp.zeros((sources, pad, width), jnp.bfloat16),
        ],
        axis=1,
    )
    got_back = lax.all_to_all(back, "ctx", split_axis=0, concat_axis=0, tiled=True)
    got_out = got_back[:, :rows_part].reshape(sources * CAP, heads_loc, tile_rows, width)
    got_lse = got_back[:, rows_part : rows_part + CAP * heads_loc].reshape(
        sources * CAP, heads_loc, width
    )
    pick_out = jnp.einsum(
        "htep,phrd->hterd", route, got_out, preferred_element_type=jnp.float32
    )
    pick_parts = jnp.einsum(
        "htep,phx->htex", route, got_lse, preferred_element_type=jnp.float32
    ).reshape(heads_loc, tiles, 2, LANE_ROWS, tile_rows)
    pick_lse = pick_parts[:, :, :, 0] + (pick_parts[:, :, :, 1] + pick_parts[:, :, :, 2])
    keep = valid[..., None]
    top = jnp.maximum(own_lse, jnp.max(jnp.where(keep, pick_lse, own_lse[:, :, None]), axis=2))
    own_w = jnp.exp(own_lse - top)
    pick_w = jnp.exp(jnp.where(keep, pick_lse - top[:, :, None], jnp.float32(-1e30)))
    numer = own_w[..., None] * own_out + jnp.sum(pick_w[..., None] * pick_out, axis=2)
    denom = own_w + jnp.sum(pick_w, axis=2)
    attention = jnp.transpose(numer / denom[..., None], (1, 2, 0, 3)).reshape(
        tokens_here, heads_loc * width
    )
    attention = attention.astype(jnp.bfloat16)
    pair = lax.axis_size("zh")
    mine_zh = lax.axis_index("zh")
    own_rows = lax.all_gather(attention, "y", axis=1, tiled=True)
    partner = lax.ppermute(attention, "zh", [(0, 1), (1, 0)])
    partner_rows = lax.all_gather(partner, "y", axis=1, tiled=True)
    groups = out_weight.reshape(-1, pair, heads_loc * width, out_weight.shape[1])
    own_w = lax.dynamic_index_in_dim(groups, mine_zh, axis=1, keepdims=False)
    partner_w = lax.dynamic_index_in_dim(groups, 1 - mine_zh, axis=1, keepdims=False)
    projected = jnp.dot(
        own_rows, own_w.reshape(-1, out_weight.shape[1]), preferred_element_type=jnp.float32
    ) + jnp.dot(
        partner_rows, partner_w.reshape(-1, out_weight.shape[1]), preferred_element_type=jnp.float32
    )
    return projected.astype(jnp.bfloat16)


def solution(mesh):
    ctx_n, head_n = mesh.devices.shape
    split = Mesh(mesh.devices.reshape(ctx_n, head_n // 2, 2), ("ctx", "y", "zh"))
    head = ("y", "zh")
    return jax.shard_map(
        local,
        mesh=split,
        in_specs=(
            P("ctx", head),
            P("ctx", head),
            P("ctx", head),
            P(head, "ctx", None),
            P(None, head),
        ),
        out_specs=P("ctx", head),
        check_vma=False,
    )
```

```python
import functools

import jax
import jax.numpy as jnp
from jax import lax
from jax.experimental import pallas as pl
from jax.experimental.pallas import tpu as pltpu
from jax.sharding import Mesh, PartitionSpec as P

CAP = 2
LANE_ROWS = 4
LSE_ROWS = 16


def split_bf16(x):
    hi = lax.reduce_precision(x, exponent_bits=8, mantissa_bits=7)
    rest = x - hi
    mid = lax.reduce_precision(rest, exponent_bits=8, mantissa_bits=7)
    lo = rest - mid
    return jnp.stack([hi, mid, lo]).astype(jnp.bfloat16)


def join_bf16(parts):
    parts = parts.astype(jnp.float32)
    return parts[0] + (parts[1] + parts[2])


def softmax_pv(scores, vals):
    top = jnp.max(scores, axis=-1)
    prob = jnp.exp(scores - top[..., None])
    total = jnp.sum(prob, axis=-1)
    part = jnp.einsum(
        "hrk,khd->hrd", prob.astype(jnp.bfloat16), vals, preferred_element_type=jnp.float32
    )
    return part / total[..., None], top + jnp.log(total)


def owner_kernel(scale, q_ref, k_ref, v_ref, part_ref, lse_ref):
    groups = q_ref.shape[0]
    slots = q_ref.shape[1]
    rows = q_ref.shape[2]
    width = q_ref.shape[3]
    heads = k_ref.shape[1] // width
    nt = (((1,), (1,)), ((), ()))
    tn = (((0,), (0,)), ((), ()))
    tail = part_ref.shape[1] - slots * rows
    part_ref[:, pl.ds(slots * rows, tail)] = jnp.zeros((groups, tail, width), part_ref.dtype)
    for j in range(slots):
        cols = pl.ds((j % heads) * width, width)
        q = q_ref[:, j].reshape(groups * rows, width)
        k = k_ref[:, cols]
        v = v_ref[:, cols]
        s_t = lax.dot_general(k, q, nt, preferred_element_type=jnp.float32) * scale
        top_t = jnp.max(s_t, axis=0, keepdims=True)
        prob_t = jnp.exp(s_t - top_t)
        total_t = jnp.sum(prob_t, axis=0, keepdims=True)
        out_t = lax.dot_general(
            v, prob_t.astype(jnp.bfloat16), tn, preferred_element_type=jnp.float32
        ) / total_t
        part_ref[:, pl.ds(j * rows, rows)] = out_t.T.reshape(groups, rows, width).astype(
            part_ref.dtype
        )
        lse_ref[pl.ds(j, 1), :] = top_t + jnp.log(total_t)


def owner_attention(got, keys, values, scale, extra):
    sources, slots, rows, width = got.shape
    step = 16
    packed = (sources, slots * rows + extra, width)
    return pl.pallas_call(
        functools.partial(owner_kernel, scale),
        grid=(sources // step,),
        in_specs=[
            pl.BlockSpec((step, slots, rows, width), lambda i: (i, 0, 0, 0)),
            pl.BlockSpec(keys.shape, lambda i: (0, 0)),
            pl.BlockSpec(values.shape, lambda i: (0, 0)),
        ],
        out_specs=[
            pl.BlockSpec((step,) + packed[1:], lambda i: (i, 0, 0)),
            pl.BlockSpec((slots, step * rows), lambda i: (0, i)),
        ],
        out_shape=[
            jax.ShapeDtypeStruct(packed, jnp.bfloat16),
            jax.ShapeDtypeStruct((slots, sources * rows), jnp.float32),
        ],
        cost_estimate=pl.CostEstimate(
            flops=6 * sources * slots * rows * keys.shape[0] * width,
            transcendentals=2 * sources * slots * rows * keys.shape[0],
            bytes_accessed=2 * got.size * 2 + 4 * slots * sources * rows,
        ),
    )(got, keys, values)


def local(queries, keys, values, selected, out_weight):
    heads_loc = selected.shape[0]
    tiles = selected.shape[1]
    tokens_here = queries.shape[0]
    width = queries.shape[1] // heads_loc
    tile_rows = tokens_here // tiles
    sources = lax.axis_size("ctx")
    mine = lax.axis_index("ctx")
    scale = width ** (-0.5)
    quer_three = queries.reshape(tokens_here, heads_loc, width)
    keys_three = keys.reshape(tokens_here, heads_loc, width)
    vals_three = values.reshape(tokens_here, heads_loc, width)

    pos = jnp.arange(tokens_here, dtype=jnp.int32)
    own_scores = (
        jnp.einsum("rhd,khd->hrk", quer_three, keys_three, preferred_element_type=jnp.float32)
        * scale
    )
    own_scores = jnp.where((pos[:, None] >= pos[None, :])[None], own_scores, jnp.float32(-1e30))
    own_out, own_lse = softmax_pv(own_scores, vals_three)
    own_out = own_out.reshape(heads_loc, tiles, tile_rows, width)
    own_lse = own_lse.reshape(heads_loc, tiles, tile_rows)

    picks = selected[:, :, 1:]
    valid = picks != mine
    target = jnp.where(valid, picks, sources)
    onehot = (target[..., None] == jnp.arange(sources, dtype=jnp.int32)).astype(jnp.int32)
    flat_hot = onehot.reshape(heads_loc, tiles * 2, sources)
    before = jnp.cumsum(flat_hot, axis=1) - flat_hot
    slot = jnp.sum(before * flat_hot, axis=-1).reshape(heads_loc, tiles, 2)
    query_src = jnp.transpose(
        quer_three.reshape(tiles, tile_rows, heads_loc, width), (2, 0, 1, 3)
    ).reshape(heads_loc, tiles, tile_rows * width)
    flat_slot = target * CAP + slot
    route = (
        flat_slot[..., None] == jnp.arange(sources * CAP, dtype=jnp.int32)
    ).astype(jnp.bfloat16)
    send_q = jnp.einsum(
        "htep,htx->phx", route, query_src, preferred_element_type=jnp.float32
    ).astype(jnp.bfloat16)
    send_q = send_q.reshape(sources, CAP, heads_loc, tile_rows, width)
    got_rows = lax.all_to_all(send_q, "ctx", split_axis=0, concat_axis=0, tiled=True)

    rows_part = CAP * heads_loc * tile_rows
    extra = -(rows_part + CAP * heads_loc) % 16 + CAP * heads_loc
    back, lse = owner_attention(
        got_rows.reshape(sources, CAP * heads_loc, tile_rows, width), keys, values, scale, extra
    )
    pieces = split_bf16(lse.reshape(CAP, heads_loc, sources, tile_rows))
    pieces = jnp.concatenate(
        [pieces, jnp.zeros((LANE_ROWS - 3,) + pieces.shape[1:], pieces.dtype)], axis=0
    )
    lse_rows = jnp.transpose(pieces, (3, 1, 2, 0, 4)).reshape(
        sources, CAP * heads_loc, LANE_ROWS * tile_rows
    )
    back = lax.dynamic_update_slice_in_dim(back, lse_rows, rows_part, axis=1)
    got_back = lax.all_to_all(back, "ctx", split_axis=0, concat_axis=0, tiled=True)
    got_out = got_back[:, :rows_part].reshape(sources * CAP, heads_loc, tile_rows, width)
    got_lse = got_back[:, rows_part : rows_part + CAP * heads_loc].reshape(
        sources * CAP, heads_loc, width
    )
    pick_out = jnp.einsum(
        "htep,phrd->hterd", route, got_out, preferred_element_type=jnp.float32
    )
    pick_parts = jnp.einsum(
        "htep,phx->htex", route, got_lse, preferred_element_type=jnp.float32
    ).reshape(heads_loc, tiles, 2, LANE_ROWS, tile_rows)
    pick_lse = pick_parts[:, :, :, 0] + (pick_parts[:, :, :, 1] + pick_parts[:, :, :, 2])
    keep = valid[..., None]
    top = jnp.maximum(own_lse, jnp.max(jnp.where(keep, pick_lse, own_lse[:, :, None]), axis=2))
    own_w = jnp.exp(own_lse - top)
    pick_w = jnp.exp(jnp.where(keep, pick_lse - top[:, :, None], jnp.float32(-1e30)))
    numer = own_w[..., None] * own_out + jnp.sum(pick_w[..., None] * pick_out, axis=2)
    denom = own_w + jnp.sum(pick_w, axis=2)
    attention = jnp.transpose(numer / denom[..., None], (1, 2, 0, 3)).reshape(
        tokens_here, heads_loc * width
    )
    attention = attention.astype(jnp.bfloat16)
    pair = lax.axis_size("zh")
    mine_zh = lax.axis_index("zh")
    own_rows = lax.all_gather(attention, "y", axis=1, tiled=True)
    partner = lax.ppermute(attention, "zh", [(0, 1), (1, 0)])
    partner_rows = lax.all_gather(partner, "y", axis=1, tiled=True)
    groups = out_weight.reshape(-1, pair, heads_loc * width, out_weight.shape[1])
    own_w = lax.dynamic_index_in_dim(groups, mine_zh, axis=1, keepdims=False)
    partner_w = lax.dynamic_index_in_dim(groups, 1 - mine_zh, axis=1, keepdims=False)
    projected = jnp.dot(
        own_rows, own_w.reshape(-1, out_weight.shape[1]), preferred_element_type=jnp.float32
    ) + jnp.dot(
        partner_rows, partner_w.reshape(-1, out_weight.shape[1]), preferred_element_type=jnp.float32
    )
    return projected.astype(jnp.bfloat16)


def solution(mesh):
    ctx_n, head_n = mesh.devices.shape
    split = Mesh(mesh.devices.reshape(ctx_n, head_n // 2, 2), ("ctx", "y", "zh"))
    head = ("y", "zh")
    return jax.shard_map(
        local,
        mesh=split,
        in_specs=(
            P("ctx", head),
            P("ctx", head),
            P("ctx", head),
            P(head, "ctx", None),
            P(None, head),
        ),
        out_specs=P("ctx", head),
        check_vma=False,
    )
```

```python
import functools

import jax
import jax.numpy as jnp
from jax import lax
from jax.experimental import pallas as pl
from jax.experimental.pallas import tpu as pltpu
from jax.sharding import Mesh, PartitionSpec as P

CAP = 2
LANE_ROWS = 4
LSE_ROWS = 16


def split_bf16(x):
    hi = lax.reduce_precision(x, exponent_bits=8, mantissa_bits=7)
    rest = x - hi
    mid = lax.reduce_precision(rest, exponent_bits=8, mantissa_bits=7)
    lo = rest - mid
    return jnp.stack([hi, mid, lo]).astype(jnp.bfloat16)


def join_bf16(parts):
    parts = parts.astype(jnp.float32)
    return parts[0] + (parts[1] + parts[2])


def softmax_pv(scores, vals):
    top = jnp.max(scores, axis=-1)
    prob = jnp.exp(scores - top[..., None])
    total = jnp.sum(prob, axis=-1)
    part = jnp.einsum(
        "hrk,khd->hrd", prob.astype(jnp.bfloat16), vals, preferred_element_type=jnp.float32
    )
    return part / total[..., None], top + jnp.log(total)


def owner_kernel(scale, q_ref, k_ref, v_ref, part_ref, lse_ref):
    groups = q_ref.shape[0]
    slots = q_ref.shape[1]
    rows = q_ref.shape[2]
    width = q_ref.shape[3]
    heads = k_ref.shape[1] // width
    nt = (((1,), (1,)), ((), ()))
    tn = (((0,), (0,)), ((), ()))
    tail = part_ref.shape[1] - slots * rows
    part_ref[:, pl.ds(slots * rows, tail)] = jnp.zeros((groups, tail, width), part_ref.dtype)
    for j in range(slots):
        cols = pl.ds((j % heads) * width, width)
        q = q_ref[:, j].reshape(groups * rows, width)
        k = k_ref[:, cols]
        v = v_ref[:, cols]
        s_t = lax.dot_general(k, q, nt, preferred_element_type=jnp.float32) * scale
        top_t = jnp.max(s_t, axis=0, keepdims=True)
        prob_t = jnp.exp(s_t - top_t)
        total_t = jnp.sum(prob_t, axis=0, keepdims=True)
        out_t = lax.dot_general(
            v, prob_t.astype(jnp.bfloat16), tn, preferred_element_type=jnp.float32
        ) / total_t
        part_ref[:, pl.ds(j * rows, rows)] = out_t.T.reshape(groups, rows, width).astype(
            part_ref.dtype
        )
        lse_ref[pl.ds(j, 1), :] = top_t + jnp.log(total_t)


def owner_attention(got, keys, values, scale, extra):
    sources, slots, rows, width = got.shape
    step = 16
    packed = (sources, slots * rows + extra, width)
    return pl.pallas_call(
        functools.partial(owner_kernel, scale),
        grid=(sources // step,),
        in_specs=[
            pl.BlockSpec((step, slots, rows, width), lambda i: (i, 0, 0, 0)),
            pl.BlockSpec(keys.shape, lambda i: (0, 0)),
            pl.BlockSpec(values.shape, lambda i: (0, 0)),
        ],
        out_specs=[
            pl.BlockSpec((step,) + packed[1:], lambda i: (i, 0, 0)),
            pl.BlockSpec((slots, step * rows), lambda i: (0, i)),
        ],
        out_shape=[
            jax.ShapeDtypeStruct(packed, jnp.bfloat16),
            jax.ShapeDtypeStruct((slots, sources * rows), jnp.float32),
        ],
        cost_estimate=pl.CostEstimate(
            flops=6 * sources * slots * rows * keys.shape[0] * width,
            transcendentals=2 * sources * slots * rows * keys.shape[0],
            bytes_accessed=2 * got.size * 2 + 4 * slots * sources * rows,
        ),
    )(got, keys, values)


def local(queries, keys, values, selected, out_weight):
    heads_loc = selected.shape[0]
    tiles = selected.shape[1]
    tokens_here = queries.shape[0]
    width = queries.shape[1] // heads_loc
    tile_rows = tokens_here // tiles
    sources = lax.axis_size("ctx")
    mine = lax.axis_index("ctx")
    scale = width ** (-0.5)
    quer_three = queries.reshape(tokens_here, heads_loc, width)
    keys_three = keys.reshape(tokens_here, heads_loc, width)
    vals_three = values.reshape(tokens_here, heads_loc, width)

    pos = jnp.arange(tokens_here, dtype=jnp.int32)
    own_scores = (
        jnp.einsum("rhd,khd->hrk", quer_three, keys_three, preferred_element_type=jnp.float32)
        * scale
    )
    own_scores = jnp.where((pos[:, None] >= pos[None, :])[None], own_scores, jnp.float32(-1e30))
    own_out, own_lse = softmax_pv(own_scores, vals_three)
    own_out = own_out.reshape(heads_loc, tiles, tile_rows, width)
    own_lse = own_lse.reshape(heads_loc, tiles, tile_rows)

    picks = selected[:, :, 1:]
    valid = picks != mine
    target = jnp.where(valid, picks, sources)
    onehot = (target[..., None] == jnp.arange(sources, dtype=jnp.int32)).astype(jnp.int32)
    flat_hot = onehot.reshape(heads_loc, tiles * 2, sources)
    before = jnp.cumsum(flat_hot, axis=1) - flat_hot
    slot = jnp.sum(before * flat_hot, axis=-1).reshape(heads_loc, tiles, 2)
    query_src = jnp.transpose(
        quer_three.reshape(tiles, tile_rows, heads_loc, width), (2, 0, 1, 3)
    ).reshape(heads_loc, tiles, tile_rows * width)
    flat_slot = target * CAP + slot
    route = (
        flat_slot[..., None] == jnp.arange(sources * CAP, dtype=jnp.int32)
    ).astype(jnp.bfloat16)
    send_q = jnp.einsum(
        "htep,htx->phx", route, query_src, preferred_element_type=jnp.float32
    ).astype(jnp.bfloat16)
    send_q = send_q.reshape(sources, CAP, heads_loc, tile_rows, width)
    got_rows = lax.all_to_all(send_q, "ctx", split_axis=0, concat_axis=0, tiled=True)

    rows_part = CAP * heads_loc * tile_rows
    extra = -(rows_part + CAP * heads_loc) % 16 + CAP * heads_loc
    back, lse = owner_attention(
        got_rows.reshape(sources, CAP * heads_loc, tile_rows, width), keys, values, scale, extra
    )
    pieces = split_bf16(lse.reshape(CAP, heads_loc, sources, tile_rows))
    pieces = jnp.concatenate(
        [pieces, jnp.zeros((LANE_ROWS - 3,) + pieces.shape[1:], pieces.dtype)], axis=0
    )
    lse_rows = jnp.transpose(pieces, (3, 1, 2, 0, 4)).reshape(
        sources, CAP * heads_loc, LANE_ROWS * tile_rows
    )
    back = lax.dynamic_update_slice_in_dim(back, lse_rows, rows_part, axis=1)
    got_back = lax.all_to_all(back, "ctx", split_axis=0, concat_axis=0, tiled=True)
    got_out = got_back[:, :rows_part].reshape(sources * CAP, heads_loc, tile_rows, width)
    got_lse = got_back[:, rows_part : rows_part + CAP * heads_loc].reshape(
        sources * CAP, heads_loc, width
    )
    pick_out = jnp.einsum(
        "htep,phrd->hterd", route, got_out, preferred_element_type=jnp.float32
    )
    pick_parts = jnp.einsum(
        "htep,phx->htex", route, got_lse, preferred_element_type=jnp.float32
    ).reshape(heads_loc, tiles, 2, LANE_ROWS, tile_rows)
    pick_lse = pick_parts[:, :, :, 0] + (pick_parts[:, :, :, 1] + pick_parts[:, :, :, 2])
    keep = valid[..., None]
    top = jnp.maximum(own_lse, jnp.max(jnp.where(keep, pick_lse, own_lse[:, :, None]), axis=2))
    own_w = jnp.exp(own_lse - top)
    pick_w = jnp.exp(jnp.where(keep, pick_lse - top[:, :, None], jnp.float32(-1e30)))
    numer = own_w[..., None] * own_out + jnp.sum(pick_w[..., None] * pick_out, axis=2)
    denom = own_w + jnp.sum(pick_w, axis=2)
    attention = jnp.transpose(numer / denom[..., None], (1, 2, 0, 3)).reshape(
        tokens_here, heads_loc * width
    )
    attention = attention.astype(jnp.bfloat16)
    pair = lax.axis_size("zh")
    mine_zh = lax.axis_index("zh")
    ring = lax.axis_size("y")
    partner = lax.ppermute(attention, "zh", [(0, 1), (1, 0)])
    both = jnp.stack([attention, partner])
    spread = jnp.broadcast_to(both[None], (ring,) + both.shape)
    got_both = lax.all_to_all(spread, "y", split_axis=0, concat_axis=0, tiled=True)
    groups = out_weight.reshape(ring, pair, heads_loc * width, out_weight.shape[1])
    own_w = lax.dynamic_index_in_dim(groups, mine_zh, axis=1, keepdims=False)
    partner_w = lax.dynamic_index_in_dim(groups, 1 - mine_zh, axis=1, keepdims=False)
    projected = jnp.einsum(
        "yrc,ycn->rn", got_both[:, 0], own_w, preferred_element_type=jnp.float32
    ) + jnp.einsum("yrc,ycn->rn", got_both[:, 1], partner_w, preferred_element_type=jnp.float32)
    return projected.astype(jnp.bfloat16)


def solution(mesh):
    ctx_n, head_n = mesh.devices.shape
    split = Mesh(mesh.devices.reshape(ctx_n, head_n // 2, 2), ("ctx", "y", "zh"))
    head = ("y", "zh")
    return jax.shard_map(
        local,
        mesh=split,
        in_specs=(
            P("ctx", head),
            P("ctx", head),
            P("ctx", head),
            P(head, "ctx", None),
            P(None, head),
        ),
        out_specs=P("ctx", head),
        check_vma=False,
    )
```

```python
import functools

import jax
import jax.numpy as jnp
from jax import lax
from jax.experimental import pallas as pl
from jax.experimental.pallas import tpu as pltpu
from jax.sharding import Mesh, PartitionSpec as P

CAP = 2
LANE_ROWS = 4
LSE_ROWS = 16


def split_bf16(x):
    hi = lax.reduce_precision(x, exponent_bits=8, mantissa_bits=7)
    rest = x - hi
    mid = lax.reduce_precision(rest, exponent_bits=8, mantissa_bits=7)
    lo = rest - mid
    return jnp.stack([hi, mid, lo]).astype(jnp.bfloat16)


def join_bf16(parts):
    parts = parts.astype(jnp.float32)
    return parts[0] + (parts[1] + parts[2])


def softmax_pv(scores, vals):
    top = jnp.max(scores, axis=-1)
    prob = jnp.exp(scores - top[..., None])
    total = jnp.sum(prob, axis=-1)
    part = jnp.einsum(
        "hrk,khd->hrd", prob.astype(jnp.bfloat16), vals, preferred_element_type=jnp.float32
    )
    return part / total[..., None], top + jnp.log(total)


def owner_kernel(scale, q_ref, k_ref, v_ref, part_ref, lse_ref):
    groups = q_ref.shape[0]
    slots = q_ref.shape[1]
    rows = q_ref.shape[2]
    width = q_ref.shape[3]
    heads = k_ref.shape[1] // width
    nt = (((1,), (1,)), ((), ()))
    tn = (((0,), (0,)), ((), ()))
    tail = part_ref.shape[1] - slots * rows
    part_ref[:, pl.ds(slots * rows, tail)] = jnp.zeros((groups, tail, width), part_ref.dtype)
    for j in range(slots):
        cols = pl.ds((j % heads) * width, width)
        q = q_ref[:, j].reshape(groups * rows, width)
        k = k_ref[:, cols]
        v = v_ref[:, cols]
        s_t = lax.dot_general(k, q, nt, preferred_element_type=jnp.float32) * scale
        top_t = jnp.max(s_t, axis=0, keepdims=True)
        prob_t = jnp.exp(s_t - top_t)
        total_t = jnp.sum(prob_t, axis=0, keepdims=True)
        out_t = lax.dot_general(
            v, prob_t.astype(jnp.bfloat16), tn, preferred_element_type=jnp.float32
        ) / total_t
        part_ref[:, pl.ds(j * rows, rows)] = out_t.T.reshape(groups, rows, width).astype(
            part_ref.dtype
        )
        lse_ref[pl.ds(j, 1), :] = top_t + jnp.log(total_t)


def owner_attention(got, keys, values, scale, extra):
    sources, slots, rows, width = got.shape
    step = 16
    packed = (sources, slots * rows + extra, width)
    return pl.pallas_call(
        functools.partial(owner_kernel, scale),
        grid=(sources // step,),
        in_specs=[
            pl.BlockSpec((step, slots, rows, width), lambda i: (i, 0, 0, 0)),
            pl.BlockSpec(keys.shape, lambda i: (0, 0)),
            pl.BlockSpec(values.shape, lambda i: (0, 0)),
        ],
        out_specs=[
            pl.BlockSpec((step,) + packed[1:], lambda i: (i, 0, 0)),
            pl.BlockSpec((slots, step * rows), lambda i: (0, i)),
        ],
        out_shape=[
            jax.ShapeDtypeStruct(packed, jnp.bfloat16),
            jax.ShapeDtypeStruct((slots, sources * rows), jnp.float32),
        ],
        cost_estimate=pl.CostEstimate(
            flops=6 * sources * slots * rows * keys.shape[0] * width,
            transcendentals=2 * sources * slots * rows * keys.shape[0],
            bytes_accessed=2 * got.size * 2 + 4 * slots * sources * rows,
        ),
    )(got, keys, values)


def local(queries, keys, values, selected, out_weight):
    heads_loc = selected.shape[0]
    tiles = selected.shape[1]
    tokens_here = queries.shape[0]
    width = queries.shape[1] // heads_loc
    tile_rows = tokens_here // tiles
    sources = lax.axis_size("ctx")
    mine = lax.axis_index("ctx")
    scale = width ** (-0.5)
    quer_three = queries.reshape(tokens_here, heads_loc, width)
    keys_three = keys.reshape(tokens_here, heads_loc, width)
    vals_three = values.reshape(tokens_here, heads_loc, width)

    pos = jnp.arange(tokens_here, dtype=jnp.int32)
    own_scores = (
        jnp.einsum("rhd,khd->hrk", quer_three, keys_three, preferred_element_type=jnp.float32)
        * scale
    )
    own_scores = jnp.where((pos[:, None] >= pos[None, :])[None], own_scores, jnp.float32(-1e30))
    own_out, own_lse = softmax_pv(own_scores, vals_three)
    own_out = own_out.reshape(heads_loc, tiles, tile_rows, width)
    own_lse = own_lse.reshape(heads_loc, tiles, tile_rows)

    picks = selected[:, :, 1:]
    valid = picks != mine
    target = jnp.where(valid, picks, sources)
    onehot = (target[..., None] == jnp.arange(sources, dtype=jnp.int32)).astype(jnp.int32)
    flat_hot = onehot.reshape(heads_loc, tiles * 2, sources)
    before = jnp.cumsum(flat_hot, axis=1) - flat_hot
    slot = jnp.sum(before * flat_hot, axis=-1).reshape(heads_loc, tiles, 2)
    query_src = jnp.transpose(
        quer_three.reshape(tiles, tile_rows, heads_loc, width), (2, 0, 1, 3)
    ).reshape(heads_loc, tiles, tile_rows * width)
    flat_slot = target * CAP + slot
    route = (
        flat_slot[..., None] == jnp.arange(sources * CAP, dtype=jnp.int32)
    ).astype(jnp.bfloat16)
    send_q = jnp.einsum(
        "htep,htx->phx", route, query_src, preferred_element_type=jnp.float32
    ).astype(jnp.bfloat16)
    send_q = send_q.reshape(sources, CAP, heads_loc, tile_rows, width)
    got_rows = lax.all_to_all(send_q, "ctx", split_axis=0, concat_axis=0, tiled=True)

    rows_part = CAP * heads_loc * tile_rows
    extra = -(rows_part + CAP * heads_loc) % 16 + CAP * heads_loc
    back, lse = owner_attention(
        got_rows.reshape(sources, CAP * heads_loc, tile_rows, width), keys, values, scale, extra
    )
    pieces = split_bf16(lse.reshape(CAP, heads_loc, sources, tile_rows))
    pieces = jnp.concatenate(
        [pieces, jnp.zeros((LANE_ROWS - 3,) + pieces.shape[1:], pieces.dtype)], axis=0
    )
    lse_rows = jnp.transpose(pieces, (3, 1, 2, 0, 4)).reshape(
        sources, CAP * heads_loc, LANE_ROWS * tile_rows
    )
    back = lax.dynamic_update_slice_in_dim(back, lse_rows, rows_part, axis=1)
    got_back = lax.all_to_all(back, "ctx", split_axis=0, concat_axis=0, tiled=True)
    got_out = got_back[:, :rows_part].reshape(sources * CAP, heads_loc, tile_rows, width)
    got_lse = got_back[:, rows_part : rows_part + CAP * heads_loc].reshape(
        sources * CAP, heads_loc, width
    )
    pick_out = jnp.einsum(
        "htep,phrd->hterd", route, got_out, preferred_element_type=jnp.float32
    )
    pick_parts = jnp.einsum(
        "htep,phx->htex", route, got_lse, preferred_element_type=jnp.float32
    ).reshape(heads_loc, tiles, 2, LANE_ROWS, tile_rows)
    pick_lse = pick_parts[:, :, :, 0] + (pick_parts[:, :, :, 1] + pick_parts[:, :, :, 2])
    keep = valid[..., None]
    top = jnp.maximum(own_lse, jnp.max(jnp.where(keep, pick_lse, own_lse[:, :, None]), axis=2))
    own_w = jnp.exp(own_lse - top)
    pick_w = jnp.exp(jnp.where(keep, pick_lse - top[:, :, None], jnp.float32(-1e30)))
    numer = own_w[..., None] * own_out + jnp.sum(pick_w[..., None] * pick_out, axis=2)
    denom = own_w + jnp.sum(pick_w, axis=2)
    attention = jnp.transpose(numer / denom[..., None], (1, 2, 0, 3)).reshape(
        tokens_here, heads_loc * width
    )
    attention = attention.astype(jnp.bfloat16)
    pair = lax.axis_size("zh")
    mine_zh = lax.axis_index("zh")
    ring = lax.axis_size("y")
    partner = lax.ppermute(attention, "zh", [(0, 1), (1, 0)])
    got_own = lax.all_to_all(
        jnp.broadcast_to(attention[None], (ring,) + attention.shape),
        "y",
        split_axis=0,
        concat_axis=0,
        tiled=True,
    )
    got_partner = lax.all_to_all(
        jnp.broadcast_to(partner[None], (ring,) + partner.shape),
        "y",
        split_axis=0,
        concat_axis=0,
        tiled=True,
    )
    groups = out_weight.reshape(ring, pair, heads_loc * width, out_weight.shape[1])
    own_w = lax.dynamic_index_in_dim(groups, mine_zh, axis=1, keepdims=False)
    partner_w = lax.dynamic_index_in_dim(groups, 1 - mine_zh, axis=1, keepdims=False)
    projected = jnp.einsum(
        "yrc,ycn->rn", got_own, own_w, preferred_element_type=jnp.float32
    ) + jnp.einsum("yrc,ycn->rn", got_partner, partner_w, preferred_element_type=jnp.float32)
    return projected.astype(jnp.bfloat16)


def solution(mesh):
    ctx_n, head_n = mesh.devices.shape
    split = Mesh(mesh.devices.reshape(ctx_n, head_n // 2, 2), ("ctx", "y", "zh"))
    head = ("y", "zh")
    return jax.shard_map(
        local,
        mesh=split,
        in_specs=(
            P("ctx", head),
            P("ctx", head),
            P("ctx", head),
            P(head, "ctx", None),
            P(None, head),
        ),
        out_specs=P("ctx", head),
        check_vma=False,
    )
```

```python
import functools

import jax
import jax.numpy as jnp
from jax import lax
from jax.experimental import pallas as pl
from jax.experimental.pallas import tpu as pltpu
from jax.sharding import Mesh, PartitionSpec as P

CAP = 2
LANE_ROWS = 4
LSE_ROWS = 16


def split_bf16(x):
    hi = lax.reduce_precision(x, exponent_bits=8, mantissa_bits=7)
    rest = x - hi
    mid = lax.reduce_precision(rest, exponent_bits=8, mantissa_bits=7)
    lo = rest - mid
    return jnp.stack([hi, mid, lo]).astype(jnp.bfloat16)


def join_bf16(parts):
    parts = parts.astype(jnp.float32)
    return parts[0] + (parts[1] + parts[2])


def softmax_pv(scores, vals):
    top = jnp.max(scores, axis=-1)
    prob = jnp.exp(scores - top[..., None])
    total = jnp.sum(prob, axis=-1)
    part = jnp.einsum(
        "hrk,khd->hrd", prob.astype(jnp.bfloat16), vals, preferred_element_type=jnp.float32
    )
    return part / total[..., None], top + jnp.log(total)


def owner_kernel(scale, q_ref, k_ref, v_ref, part_ref, lse_ref):
    groups = q_ref.shape[0]
    slots = q_ref.shape[1]
    rows = q_ref.shape[2]
    width = q_ref.shape[3]
    heads = k_ref.shape[1] // width
    nt = (((1,), (1,)), ((), ()))
    tn = (((0,), (0,)), ((), ()))
    tail = part_ref.shape[1] - slots * rows
    part_ref[:, pl.ds(slots * rows, tail)] = jnp.zeros((groups, tail, width), part_ref.dtype)
    for j in range(slots):
        cols = pl.ds((j % heads) * width, width)
        q = q_ref[:, j].reshape(groups * rows, width)
        k = k_ref[:, cols]
        v = v_ref[:, cols]
        s_t = lax.dot_general(k, q, nt, preferred_element_type=jnp.float32) * scale
        top_t = jnp.max(s_t, axis=0, keepdims=True)
        prob_t = jnp.exp(s_t - top_t)
        total_t = jnp.sum(prob_t, axis=0, keepdims=True)
        out_t = lax.dot_general(
            v, prob_t.astype(jnp.bfloat16), tn, preferred_element_type=jnp.float32
        ) / total_t
        part_ref[:, pl.ds(j * rows, rows)] = out_t.T.reshape(groups, rows, width).astype(
            part_ref.dtype
        )
        lse_ref[pl.ds(j, 1), :] = top_t + jnp.log(total_t)


def owner_attention(got, keys, values, scale, extra):
    sources, slots, rows, width = got.shape
    step = 16
    packed = (sources, slots * rows + extra, width)
    return pl.pallas_call(
        functools.partial(owner_kernel, scale),
        grid=(sources // step,),
        in_specs=[
            pl.BlockSpec((step, slots, rows, width), lambda i: (i, 0, 0, 0)),
            pl.BlockSpec(keys.shape, lambda i: (0, 0)),
            pl.BlockSpec(values.shape, lambda i: (0, 0)),
        ],
        out_specs=[
            pl.BlockSpec((step,) + packed[1:], lambda i: (i, 0, 0)),
            pl.BlockSpec((slots, step * rows), lambda i: (0, i)),
        ],
        out_shape=[
            jax.ShapeDtypeStruct(packed, jnp.bfloat16),
            jax.ShapeDtypeStruct((slots, sources * rows), jnp.float32),
        ],
        cost_estimate=pl.CostEstimate(
            flops=6 * sources * slots * rows * keys.shape[0] * width,
            transcendentals=2 * sources * slots * rows * keys.shape[0],
            bytes_accessed=2 * got.size * 2 + 4 * slots * sources * rows,
        ),
    )(got, keys, values)


def local(queries, keys, values, selected, out_weight):
    heads_loc = selected.shape[0]
    tiles = selected.shape[1]
    tokens_here = queries.shape[0]
    width = queries.shape[1] // heads_loc
    tile_rows = tokens_here // tiles
    sources = lax.axis_size("ctx")
    mine = lax.axis_index("ctx")
    scale = width ** (-0.5)
    quer_three = queries.reshape(tokens_here, heads_loc, width)
    keys_three = keys.reshape(tokens_here, heads_loc, width)
    vals_three = values.reshape(tokens_here, heads_loc, width)

    pos = jnp.arange(tokens_here, dtype=jnp.int32)
    own_scores = (
        jnp.einsum("rhd,khd->hrk", quer_three, keys_three, preferred_element_type=jnp.float32)
        * scale
    )
    own_scores = jnp.where((pos[:, None] >= pos[None, :])[None], own_scores, jnp.float32(-1e30))
    own_out, own_lse = softmax_pv(own_scores, vals_three)
    own_out = own_out.reshape(heads_loc, tiles, tile_rows, width)
    own_lse = own_lse.reshape(heads_loc, tiles, tile_rows)

    picks = selected[:, :, 1:]
    valid = picks != mine
    target = jnp.where(valid, picks, sources)
    onehot = (target[..., None] == jnp.arange(sources, dtype=jnp.int32)).astype(jnp.int32)
    flat_hot = onehot.reshape(heads_loc, tiles * 2, sources)
    before = jnp.cumsum(flat_hot, axis=1) - flat_hot
    slot = jnp.sum(before * flat_hot, axis=-1).reshape(heads_loc, tiles, 2)
    query_src = jnp.transpose(
        quer_three.reshape(tiles, tile_rows, heads_loc, width), (2, 0, 1, 3)
    ).reshape(heads_loc, tiles, tile_rows * width)
    flat_slot = target * CAP + slot
    route = (
        flat_slot[..., None] == jnp.arange(sources * CAP, dtype=jnp.int32)
    ).astype(jnp.bfloat16)
    send_q = jnp.einsum(
        "htep,htx->phx", route, query_src, preferred_element_type=jnp.float32
    ).astype(jnp.bfloat16)
    send_q = send_q.reshape(sources, CAP, heads_loc, tile_rows, width)
    got_rows = lax.all_to_all(send_q, "ctx", split_axis=0, concat_axis=0, tiled=True)

    rows_part = CAP * heads_loc * tile_rows
    extra = -(rows_part + CAP * heads_loc) % 16 + CAP * heads_loc
    back, lse = owner_attention(
        got_rows.reshape(sources, CAP * heads_loc, tile_rows, width), keys, values, scale, extra
    )
    pieces = split_bf16(lse.reshape(CAP, heads_loc, sources, tile_rows))
    pieces = jnp.concatenate(
        [pieces, jnp.zeros((LANE_ROWS - 3,) + pieces.shape[1:], pieces.dtype)], axis=0
    )
    lse_rows = jnp.transpose(pieces, (3, 1, 2, 0, 4)).reshape(
        sources, CAP * heads_loc, LANE_ROWS * tile_rows
    )
    back = lax.dynamic_update_slice_in_dim(back, lse_rows, rows_part, axis=1)
    got_back = lax.all_to_all(back, "ctx", split_axis=0, concat_axis=0, tiled=True)
    got_out = got_back[:, :rows_part].reshape(sources * CAP, heads_loc, tile_rows, width)
    got_lse = got_back[:, rows_part : rows_part + CAP * heads_loc].reshape(
        sources * CAP, heads_loc, width
    )
    pick_out = jnp.einsum(
        "htep,phrd->hterd", route, got_out, preferred_element_type=jnp.float32
    )
    pick_parts = jnp.einsum(
        "htep,phx->htex", route, got_lse, preferred_element_type=jnp.float32
    ).reshape(heads_loc, tiles, 2, LANE_ROWS, tile_rows)
    pick_lse = pick_parts[:, :, :, 0] + (pick_parts[:, :, :, 1] + pick_parts[:, :, :, 2])
    keep = valid[..., None]
    top = jnp.maximum(own_lse, jnp.max(jnp.where(keep, pick_lse, own_lse[:, :, None]), axis=2))
    own_w = jnp.exp(own_lse - top)
    pick_w = jnp.exp(jnp.where(keep, pick_lse - top[:, :, None], jnp.float32(-1e30)))
    numer = own_w[..., None] * own_out + jnp.sum(pick_w[..., None] * pick_out, axis=2)
    denom = own_w + jnp.sum(pick_w, axis=2)
    attention = jnp.transpose(numer / denom[..., None], (1, 2, 0, 3)).reshape(
        tokens_here, heads_loc * width
    )
    attention = attention.astype(jnp.bfloat16)
    pair = lax.axis_size("zh")
    ring = lax.axis_size("y")
    both = lax.all_to_all(
        jnp.broadcast_to(attention[None], (pair,) + attention.shape),
        "zh",
        split_axis=0,
        concat_axis=0,
        tiled=True,
    )
    every = lax.all_to_all(
        jnp.broadcast_to(both[None], (ring,) + both.shape),
        "y",
        split_axis=0,
        concat_axis=0,
        tiled=True,
    )
    projected = jnp.einsum(
        "yzrc,yzcn->rn",
        every,
        out_weight.reshape(ring, pair, heads_loc * width, out_weight.shape[1]),
        preferred_element_type=jnp.float32,
    )
    return projected.astype(jnp.bfloat16)


def solution(mesh):
    ctx_n, head_n = mesh.devices.shape
    split = Mesh(mesh.devices.reshape(ctx_n, head_n // 2, 2), ("ctx", "y", "zh"))
    head = ("y", "zh")
    return jax.shard_map(
        local,
        mesh=split,
        in_specs=(
            P("ctx", head),
            P("ctx", head),
            P("ctx", head),
            P(head, "ctx", None),
            P(None, head),
        ),
        out_specs=P("ctx", head),
        check_vma=False,
    )
```

```python
import functools

import jax
import jax.numpy as jnp
from jax import lax
from jax.experimental import pallas as pl
from jax.experimental.pallas import tpu as pltpu
from jax.sharding import Mesh, PartitionSpec as P

CAP = 2
LANE_ROWS = 4
LSE_ROWS = 16


def split_bf16(x):
    hi = lax.reduce_precision(x, exponent_bits=8, mantissa_bits=7)
    rest = x - hi
    mid = lax.reduce_precision(rest, exponent_bits=8, mantissa_bits=7)
    lo = rest - mid
    return jnp.stack([hi, mid, lo]).astype(jnp.bfloat16)


def join_bf16(parts):
    parts = parts.astype(jnp.float32)
    return parts[0] + (parts[1] + parts[2])


def softmax_pv(scores, vals):
    top = jnp.max(scores, axis=-1)
    prob = jnp.exp(scores - top[..., None])
    total = jnp.sum(prob, axis=-1)
    part = jnp.einsum(
        "hrk,khd->hrd", prob.astype(jnp.bfloat16), vals, preferred_element_type=jnp.float32
    )
    return part / total[..., None], top + jnp.log(total)


def owner_kernel(scale, q_ref, k_ref, v_ref, part_ref, lse_ref):
    groups = q_ref.shape[0]
    slots = q_ref.shape[1]
    rows = q_ref.shape[2]
    width = q_ref.shape[3]
    heads = k_ref.shape[1] // width
    nt = (((1,), (1,)), ((), ()))
    tn = (((0,), (0,)), ((), ()))
    tail = part_ref.shape[1] - slots * rows
    part_ref[:, pl.ds(slots * rows, tail)] = jnp.zeros((groups, tail, width), part_ref.dtype)
    for j in range(slots):
        cols = pl.ds((j % heads) * width, width)
        q = q_ref[:, j].reshape(groups * rows, width)
        k = k_ref[:, cols]
        v = v_ref[:, cols]
        s_t = lax.dot_general(k, q, nt, preferred_element_type=jnp.float32) * scale
        top_t = jnp.max(s_t, axis=0, keepdims=True)
        prob_t = jnp.exp(s_t - top_t)
        total_t = jnp.sum(prob_t, axis=0, keepdims=True)
        out_t = lax.dot_general(
            v, prob_t.astype(jnp.bfloat16), tn, preferred_element_type=jnp.float32
        ) / total_t
        part_ref[:, pl.ds(j * rows, rows)] = out_t.T.reshape(groups, rows, width).astype(
            part_ref.dtype
        )
        lse_ref[pl.ds(j, 1), :] = top_t + jnp.log(total_t)


def owner_attention(got, keys, values, scale, extra):
    sources, slots, rows, width = got.shape
    step = 32
    packed = (sources, slots * rows + extra, width)
    return pl.pallas_call(
        functools.partial(owner_kernel, scale),
        grid=(sources // step,),
        in_specs=[
            pl.BlockSpec((step, slots, rows, width), lambda i: (i, 0, 0, 0)),
            pl.BlockSpec(keys.shape, lambda i: (0, 0)),
            pl.BlockSpec(values.shape, lambda i: (0, 0)),
        ],
        out_specs=[
            pl.BlockSpec((step,) + packed[1:], lambda i: (i, 0, 0)),
            pl.BlockSpec((slots, step * rows), lambda i: (0, i)),
        ],
        out_shape=[
            jax.ShapeDtypeStruct(packed, jnp.bfloat16),
            jax.ShapeDtypeStruct((slots, sources * rows), jnp.float32),
        ],
        cost_estimate=pl.CostEstimate(
            flops=6 * sources * slots * rows * keys.shape[0] * width,
            transcendentals=2 * sources * slots * rows * keys.shape[0],
            bytes_accessed=2 * got.size * 2 + 4 * slots * sources * rows,
        ),
    )(got, keys, values)


def local(queries, keys, values, selected, out_weight):
    heads_loc = selected.shape[0]
    tiles = selected.shape[1]
    tokens_here = queries.shape[0]
    width = queries.shape[1] // heads_loc
    tile_rows = tokens_here // tiles
    sources = lax.axis_size("ctx")
    mine = lax.axis_index("ctx")
    scale = width ** (-0.5)
    quer_three = queries.reshape(tokens_here, heads_loc, width)
    keys_three = keys.reshape(tokens_here, heads_loc, width)
    vals_three = values.reshape(tokens_here, heads_loc, width)

    pos = jnp.arange(tokens_here, dtype=jnp.int32)
    own_scores = (
        jnp.einsum("rhd,khd->hrk", quer_three, keys_three, preferred_element_type=jnp.float32)
        * scale
    )
    own_scores = jnp.where((pos[:, None] >= pos[None, :])[None], own_scores, jnp.float32(-1e30))
    own_out, own_lse = softmax_pv(own_scores, vals_three)
    own_out = own_out.reshape(heads_loc, tiles, tile_rows, width)
    own_lse = own_lse.reshape(heads_loc, tiles, tile_rows)

    picks = selected[:, :, 1:]
    valid = picks != mine
    target = jnp.where(valid, picks, sources)
    onehot = (target[..., None] == jnp.arange(sources, dtype=jnp.int32)).astype(jnp.int32)
    flat_hot = onehot.reshape(heads_loc, tiles * 2, sources)
    before = jnp.cumsum(flat_hot, axis=1) - flat_hot
    slot = jnp.sum(before * flat_hot, axis=-1).reshape(heads_loc, tiles, 2)
    query_src = jnp.transpose(
        quer_three.reshape(tiles, tile_rows, heads_loc, width), (2, 0, 1, 3)
    ).reshape(heads_loc, tiles, tile_rows * width)
    flat_slot = target * CAP + slot
    route = (
        flat_slot[..., None] == jnp.arange(sources * CAP, dtype=jnp.int32)
    ).astype(jnp.bfloat16)
    send_q = jnp.einsum(
        "htep,htx->phx", route, query_src, preferred_element_type=jnp.float32
    ).astype(jnp.bfloat16)
    send_q = send_q.reshape(sources, CAP, heads_loc, tile_rows, width)
    got_rows = lax.all_to_all(send_q, "ctx", split_axis=0, concat_axis=0, tiled=True)

    rows_part = CAP * heads_loc * tile_rows
    extra = -(rows_part + CAP * heads_loc) % 16 + CAP * heads_loc
    back, lse = owner_attention(
        got_rows.reshape(sources, CAP * heads_loc, tile_rows, width), keys, values, scale, extra
    )
    pieces = split_bf16(lse.reshape(CAP, heads_loc, sources, tile_rows))
    pieces = jnp.concatenate(
        [pieces, jnp.zeros((LANE_ROWS - 3,) + pieces.shape[1:], pieces.dtype)], axis=0
    )
    lse_rows = jnp.transpose(pieces, (3, 1, 2, 0, 4)).reshape(
        sources, CAP * heads_loc, LANE_ROWS * tile_rows
    )
    back = lax.dynamic_update_slice_in_dim(back, lse_rows, rows_part, axis=1)
    got_back = lax.all_to_all(back, "ctx", split_axis=0, concat_axis=0, tiled=True)
    got_out = got_back[:, :rows_part].reshape(sources * CAP, heads_loc, tile_rows, width)
    got_lse = got_back[:, rows_part : rows_part + CAP * heads_loc].reshape(
        sources * CAP, heads_loc, width
    )
    pick_out = jnp.einsum(
        "htep,phrd->hterd", route, got_out, preferred_element_type=jnp.float32
    )
    pick_parts = jnp.einsum(
        "htep,phx->htex", route, got_lse, preferred_element_type=jnp.float32
    ).reshape(heads_loc, tiles, 2, LANE_ROWS, tile_rows)
    pick_lse = pick_parts[:, :, :, 0] + (pick_parts[:, :, :, 1] + pick_parts[:, :, :, 2])
    keep = valid[..., None]
    top = jnp.maximum(own_lse, jnp.max(jnp.where(keep, pick_lse, own_lse[:, :, None]), axis=2))
    own_w = jnp.exp(own_lse - top)
    pick_w = jnp.exp(jnp.where(keep, pick_lse - top[:, :, None], jnp.float32(-1e30)))
    numer = own_w[..., None] * own_out + jnp.sum(pick_w[..., None] * pick_out, axis=2)
    denom = own_w + jnp.sum(pick_w, axis=2)
    attention = jnp.transpose(numer / denom[..., None], (1, 2, 0, 3)).reshape(
        tokens_here, heads_loc * width
    )
    attention = attention.astype(jnp.bfloat16)
    pair = lax.axis_size("zh")
    mine_zh = lax.axis_index("zh")
    ring = lax.axis_size("y")
    partner = lax.ppermute(attention, "zh", [(0, 1), (1, 0)])
    both = jnp.stack([attention, partner])
    spread = jnp.broadcast_to(both[None], (ring,) + both.shape)
    got_both = lax.all_to_all(spread, "y", split_axis=0, concat_axis=0, tiled=True)
    groups = out_weight.reshape(ring, pair, heads_loc * width, out_weight.shape[1])
    own_w = lax.dynamic_index_in_dim(groups, mine_zh, axis=1, keepdims=False)
    partner_w = lax.dynamic_index_in_dim(groups, 1 - mine_zh, axis=1, keepdims=False)
    projected = jnp.einsum(
        "yrc,ycn->rn", got_both[:, 0], own_w, preferred_element_type=jnp.float32
    ) + jnp.einsum("yrc,ycn->rn", got_both[:, 1], partner_w, preferred_element_type=jnp.float32)
    return projected.astype(jnp.bfloat16)


def solution(mesh):
    ctx_n, head_n = mesh.devices.shape
    split = Mesh(mesh.devices.reshape(ctx_n, head_n // 2, 2), ("ctx", "y", "zh"))
    head = ("y", "zh")
    return jax.shard_map(
        local,
        mesh=split,
        in_specs=(
            P("ctx", head),
            P("ctx", head),
            P("ctx", head),
            P(head, "ctx", None),
            P(None, head),
        ),
        out_specs=P("ctx", head),
        check_vma=False,
    )
```

```python
import functools

import jax
import jax.numpy as jnp
from jax import lax
from jax.experimental import pallas as pl
from jax.experimental.pallas import tpu as pltpu
from jax.sharding import Mesh, PartitionSpec as P

CAP = 2
LANE_ROWS = 4
LSE_ROWS = 16


def split_bf16(x):
    hi = lax.reduce_precision(x, exponent_bits=8, mantissa_bits=7)
    rest = x - hi
    mid = lax.reduce_precision(rest, exponent_bits=8, mantissa_bits=7)
    lo = rest - mid
    return jnp.stack([hi, mid, lo]).astype(jnp.bfloat16)


def join_bf16(parts):
    parts = parts.astype(jnp.float32)
    return parts[0] + (parts[1] + parts[2])


def softmax_pv(scores, vals):
    top = jnp.max(scores, axis=-1)
    prob = jnp.exp(scores - top[..., None])
    total = jnp.sum(prob, axis=-1)
    part = jnp.einsum(
        "hrk,khd->hrd", prob.astype(jnp.bfloat16), vals, preferred_element_type=jnp.float32
    )
    return part / total[..., None], top + jnp.log(total)


def owner_kernel(scale, q_ref, k_ref, v_ref, part_ref, lse_ref):
    groups = q_ref.shape[0]
    slots = q_ref.shape[1]
    rows = q_ref.shape[2]
    width = q_ref.shape[3]
    heads = k_ref.shape[1] // width
    nt = (((1,), (1,)), ((), ()))
    tn = (((0,), (0,)), ((), ()))
    tail = part_ref.shape[1] - slots * rows
    part_ref[:, pl.ds(slots * rows, tail)] = jnp.zeros((groups, tail, width), part_ref.dtype)
    for j in range(slots):
        cols = pl.ds((j % heads) * width, width)
        q = q_ref[:, j].reshape(groups * rows, width)
        k = k_ref[:, cols]
        v = v_ref[:, cols]
        s_t = lax.dot_general(k, q, nt, preferred_element_type=jnp.float32) * scale
        top_t = jnp.max(s_t, axis=0, keepdims=True)
        prob_t = jnp.exp(s_t - top_t)
        total_t = jnp.sum(prob_t, axis=0, keepdims=True)
        out_t = lax.dot_general(
            v, prob_t.astype(jnp.bfloat16), tn, preferred_element_type=jnp.float32
        ) / total_t
        part_ref[:, pl.ds(j * rows, rows)] = out_t.T.reshape(groups, rows, width).astype(
            part_ref.dtype
        )
        lse_ref[pl.ds(j, 1), :] = top_t + jnp.log(total_t)


def owner_attention(got, keys, values, scale, extra):
    sources, slots, rows, width = got.shape
    step = 64
    packed = (sources, slots * rows + extra, width)
    return pl.pallas_call(
        functools.partial(owner_kernel, scale),
        grid=(sources // step,),
        in_specs=[
            pl.BlockSpec((step, slots, rows, width), lambda i: (i, 0, 0, 0)),
            pl.BlockSpec(keys.shape, lambda i: (0, 0)),
            pl.BlockSpec(values.shape, lambda i: (0, 0)),
        ],
        out_specs=[
            pl.BlockSpec((step,) + packed[1:], lambda i: (i, 0, 0)),
            pl.BlockSpec((slots, step * rows), lambda i: (0, i)),
        ],
        out_shape=[
            jax.ShapeDtypeStruct(packed, jnp.bfloat16),
            jax.ShapeDtypeStruct((slots, sources * rows), jnp.float32),
        ],
        cost_estimate=pl.CostEstimate(
            flops=6 * sources * slots * rows * keys.shape[0] * width,
            transcendentals=2 * sources * slots * rows * keys.shape[0],
            bytes_accessed=2 * got.size * 2 + 4 * slots * sources * rows,
        ),
    )(got, keys, values)


def local(queries, keys, values, selected, out_weight):
    heads_loc = selected.shape[0]
    tiles = selected.shape[1]
    tokens_here = queries.shape[0]
    width = queries.shape[1] // heads_loc
    tile_rows = tokens_here // tiles
    sources = lax.axis_size("ctx")
    mine = lax.axis_index("ctx")
    scale = width ** (-0.5)
    quer_three = queries.reshape(tokens_here, heads_loc, width)
    keys_three = keys.reshape(tokens_here, heads_loc, width)
    vals_three = values.reshape(tokens_here, heads_loc, width)

    pos = jnp.arange(tokens_here, dtype=jnp.int32)
    own_scores = (
        jnp.einsum("rhd,khd->hrk", quer_three, keys_three, preferred_element_type=jnp.float32)
        * scale
    )
    own_scores = jnp.where((pos[:, None] >= pos[None, :])[None], own_scores, jnp.float32(-1e30))
    own_out, own_lse = softmax_pv(own_scores, vals_three)
    own_out = own_out.reshape(heads_loc, tiles, tile_rows, width)
    own_lse = own_lse.reshape(heads_loc, tiles, tile_rows)

    picks = selected[:, :, 1:]
    valid = picks != mine
    target = jnp.where(valid, picks, sources)
    onehot = (target[..., None] == jnp.arange(sources, dtype=jnp.int32)).astype(jnp.int32)
    flat_hot = onehot.reshape(heads_loc, tiles * 2, sources)
    before = jnp.cumsum(flat_hot, axis=1) - flat_hot
    slot = jnp.sum(before * flat_hot, axis=-1).reshape(heads_loc, tiles, 2)
    query_src = jnp.transpose(
        quer_three.reshape(tiles, tile_rows, heads_loc, width), (2, 0, 1, 3)
    ).reshape(heads_loc, tiles, tile_rows * width)
    flat_slot = target * CAP + slot
    route = (
        flat_slot[..., None] == jnp.arange(sources * CAP, dtype=jnp.int32)
    ).astype(jnp.bfloat16)
    send_q = jnp.einsum(
        "htep,htx->phx", route, query_src, preferred_element_type=jnp.float32
    ).astype(jnp.bfloat16)
    send_q = send_q.reshape(sources, CAP, heads_loc, tile_rows, width)
    got_rows = lax.all_to_all(send_q, "ctx", split_axis=0, concat_axis=0, tiled=True)

    rows_part = CAP * heads_loc * tile_rows
    extra = -(rows_part + CAP * heads_loc) % 16 + CAP * heads_loc
    back, lse = owner_attention(
        got_rows.reshape(sources, CAP * heads_loc, tile_rows, width), keys, values, scale, extra
    )
    pieces = split_bf16(lse.reshape(CAP, heads_loc, sources, tile_rows))
    pieces = jnp.concatenate(
        [pieces, jnp.zeros((LANE_ROWS - 3,) + pieces.shape[1:], pieces.dtype)], axis=0
    )
    lse_rows = jnp.transpose(pieces, (3, 1, 2, 0, 4)).reshape(
        sources, CAP * heads_loc, LANE_ROWS * tile_rows
    )
    back = lax.dynamic_update_slice_in_dim(back, lse_rows, rows_part, axis=1)
    got_back = lax.all_to_all(back, "ctx", split_axis=0, concat_axis=0, tiled=True)
    got_out = got_back[:, :rows_part].reshape(sources * CAP, heads_loc, tile_rows, width)
    got_lse = got_back[:, rows_part : rows_part + CAP * heads_loc].reshape(
        sources * CAP, heads_loc, width
    )
    pick_out = jnp.einsum(
        "htep,phrd->hterd", route, got_out, preferred_element_type=jnp.float32
    )
    pick_parts = jnp.einsum(
        "htep,phx->htex", route, got_lse, preferred_element_type=jnp.float32
    ).reshape(heads_loc, tiles, 2, LANE_ROWS, tile_rows)
    pick_lse = pick_parts[:, :, :, 0] + (pick_parts[:, :, :, 1] + pick_parts[:, :, :, 2])
    keep = valid[..., None]
    top = jnp.maximum(own_lse, jnp.max(jnp.where(keep, pick_lse, own_lse[:, :, None]), axis=2))
    own_w = jnp.exp(own_lse - top)
    pick_w = jnp.exp(jnp.where(keep, pick_lse - top[:, :, None], jnp.float32(-1e30)))
    numer = own_w[..., None] * own_out + jnp.sum(pick_w[..., None] * pick_out, axis=2)
    denom = own_w + jnp.sum(pick_w, axis=2)
    attention = jnp.transpose(numer / denom[..., None], (1, 2, 0, 3)).reshape(
        tokens_here, heads_loc * width
    )
    attention = attention.astype(jnp.bfloat16)
    pair = lax.axis_size("zh")
    mine_zh = lax.axis_index("zh")
    ring = lax.axis_size("y")
    partner = lax.ppermute(attention, "zh", [(0, 1), (1, 0)])
    both = jnp.stack([attention, partner])
    spread = jnp.broadcast_to(both[None], (ring,) + both.shape)
    got_both = lax.all_to_all(spread, "y", split_axis=0, concat_axis=0, tiled=True)
    groups = out_weight.reshape(ring, pair, heads_loc * width, out_weight.shape[1])
    own_w = lax.dynamic_index_in_dim(groups, mine_zh, axis=1, keepdims=False)
    partner_w = lax.dynamic_index_in_dim(groups, 1 - mine_zh, axis=1, keepdims=False)
    projected = jnp.einsum(
        "yrc,ycn->rn", got_both[:, 0], own_w, preferred_element_type=jnp.float32
    ) + jnp.einsum("yrc,ycn->rn", got_both[:, 1], partner_w, preferred_element_type=jnp.float32)
    return projected.astype(jnp.bfloat16)


def solution(mesh):
    ctx_n, head_n = mesh.devices.shape
    split = Mesh(mesh.devices.reshape(ctx_n, head_n // 2, 2), ("ctx", "y", "zh"))
    head = ("y", "zh")
    return jax.shard_map(
        local,
        mesh=split,
        in_specs=(
            P("ctx", head),
            P("ctx", head),
            P("ctx", head),
            P(head, "ctx", None),
            P(None, head),
        ),
        out_specs=P("ctx", head),
        check_vma=False,
    )
```

```python
import functools

import jax
import jax.numpy as jnp
from jax import lax
from jax.experimental import pallas as pl
from jax.experimental.pallas import tpu as pltpu
from jax.sharding import Mesh, PartitionSpec as P

CAP = 2
LANE_ROWS = 4
LSE_ROWS = 16


def split_bf16(x):
    hi = lax.reduce_precision(x, exponent_bits=8, mantissa_bits=7)
    rest = x - hi
    mid = lax.reduce_precision(rest, exponent_bits=8, mantissa_bits=7)
    lo = rest - mid
    return jnp.stack([hi, mid, lo]).astype(jnp.bfloat16)


def join_bf16(parts):
    parts = parts.astype(jnp.float32)
    return parts[0] + (parts[1] + parts[2])


def softmax_pv(scores, vals):
    top = jnp.max(scores, axis=-1)
    prob = jnp.exp(scores - top[..., None])
    total = jnp.sum(prob, axis=-1)
    part = jnp.einsum(
        "hrk,khd->hrd", prob.astype(jnp.bfloat16), vals, preferred_element_type=jnp.float32
    )
    return part / total[..., None], top + jnp.log(total)


def owner_kernel(scale, q_ref, k_ref, v_ref, part_ref, lse_ref):
    groups = q_ref.shape[0]
    slots = q_ref.shape[1]
    rows = q_ref.shape[2]
    width = q_ref.shape[3]
    heads = k_ref.shape[1] // width
    nt = (((1,), (1,)), ((), ()))
    tn = (((0,), (0,)), ((), ()))
    tail = part_ref.shape[1] - slots * rows
    part_ref[:, pl.ds(slots * rows, tail)] = jnp.zeros((groups, tail, width), part_ref.dtype)
    for j in range(slots):
        cols = pl.ds((j % heads) * width, width)
        q = q_ref[:, j].reshape(groups * rows, width)
        k = k_ref[:, cols]
        v = v_ref[:, cols]
        s_t = lax.dot_general(k, q, nt, preferred_element_type=jnp.float32) * scale
        top_t = jnp.max(s_t, axis=0, keepdims=True)
        prob_t = jnp.exp(s_t - top_t)
        total_t = jnp.sum(prob_t, axis=0, keepdims=True)
        out_t = lax.dot_general(
            v, prob_t.astype(jnp.bfloat16), tn, preferred_element_type=jnp.float32
        ) / total_t
        part_ref[:, pl.ds(j * rows, rows)] = out_t.T.reshape(groups, rows, width).astype(
            part_ref.dtype
        )
        lse_ref[pl.ds(j, 1), :] = top_t + jnp.log(total_t)


def owner_attention(got, keys, values, scale, extra):
    sources, slots, rows, width = got.shape
    step = 64
    packed = (sources, slots * rows + extra, width)
    return pl.pallas_call(
        functools.partial(owner_kernel, scale),
        grid=(sources // step,),
        in_specs=[
            pl.BlockSpec((step, slots, rows, width), lambda i: (i, 0, 0, 0)),
            pl.BlockSpec(keys.shape, lambda i: (0, 0)),
            pl.BlockSpec(values.shape, lambda i: (0, 0)),
        ],
        out_specs=[
            pl.BlockSpec((step,) + packed[1:], lambda i: (i, 0, 0)),
            pl.BlockSpec((slots, step * rows), lambda i: (0, i)),
        ],
        out_shape=[
            jax.ShapeDtypeStruct(packed, jnp.bfloat16),
            jax.ShapeDtypeStruct((slots, sources * rows), jnp.float32),
        ],
        cost_estimate=pl.CostEstimate(
            flops=6 * sources * slots * rows * keys.shape[0] * width,
            transcendentals=2 * sources * slots * rows * keys.shape[0],
            bytes_accessed=2 * got.size * 2 + 4 * slots * sources * rows,
        ),
    )(got, keys, values)


def local(queries, keys, values, selected, out_weight):
    heads_loc = selected.shape[0]
    tiles = selected.shape[1]
    tokens_here = queries.shape[0]
    width = queries.shape[1] // heads_loc
    tile_rows = tokens_here // tiles
    sources = lax.axis_size("ctx")
    mine = lax.axis_index("ctx")
    scale = width ** (-0.5)
    quer_three = queries.reshape(tokens_here, heads_loc, width)
    keys_three = keys.reshape(tokens_here, heads_loc, width)
    vals_three = values.reshape(tokens_here, heads_loc, width)

    pos = jnp.arange(tokens_here, dtype=jnp.int32)
    own_scores = (
        jnp.einsum("rhd,khd->hrk", quer_three, keys_three, preferred_element_type=jnp.float32)
        * scale
    )
    own_scores = jnp.where((pos[:, None] >= pos[None, :])[None], own_scores, jnp.float32(-1e30))
    own_out, own_lse = softmax_pv(own_scores, vals_three)
    own_out = own_out.reshape(heads_loc, tiles, tile_rows, width)
    own_lse = own_lse.reshape(heads_loc, tiles, tile_rows)

    picks = selected[:, :, 1:]
    valid = picks != mine
    target = jnp.where(valid, picks, sources)
    onehot = (target[..., None] == jnp.arange(sources, dtype=jnp.int32)).astype(jnp.int32)
    flat_hot = onehot.reshape(heads_loc, tiles * 2, sources)
    before = jnp.cumsum(flat_hot, axis=1) - flat_hot
    slot = jnp.sum(before * flat_hot, axis=-1).reshape(heads_loc, tiles, 2)
    flat_slot = target * CAP + slot
    route = (
        flat_slot[..., None] == jnp.arange(sources * CAP, dtype=jnp.int32)
    ).astype(jnp.bfloat16)
    send_q = jnp.einsum(
        "htep,trhd->phrd",
        route,
        quer_three.reshape(tiles, tile_rows, heads_loc, width),
        preferred_element_type=jnp.float32,
    ).astype(jnp.bfloat16)
    send_q = send_q.reshape(sources, CAP, heads_loc, tile_rows, width)
    got_rows = lax.all_to_all(send_q, "ctx", split_axis=0, concat_axis=0, tiled=True)

    rows_part = CAP * heads_loc * tile_rows
    extra = -(rows_part + CAP * heads_loc) % 16 + CAP * heads_loc
    back, lse = owner_attention(
        got_rows.reshape(sources, CAP * heads_loc, tile_rows, width), keys, values, scale, extra
    )
    pieces = split_bf16(lse.reshape(CAP, heads_loc, sources, tile_rows))
    pieces = jnp.concatenate(
        [pieces, jnp.zeros((LANE_ROWS - 3,) + pieces.shape[1:], pieces.dtype)], axis=0
    )
    lse_rows = jnp.transpose(pieces, (3, 1, 2, 0, 4)).reshape(
        sources, CAP * heads_loc, LANE_ROWS * tile_rows
    )
    back = lax.dynamic_update_slice_in_dim(back, lse_rows, rows_part, axis=1)
    got_back = lax.all_to_all(back, "ctx", split_axis=0, concat_axis=0, tiled=True)
    got_out = got_back[:, :rows_part].reshape(sources * CAP, heads_loc, tile_rows, width)
    got_lse = got_back[:, rows_part : rows_part + CAP * heads_loc].reshape(
        sources * CAP, heads_loc, width
    )
    pick_out = jnp.einsum(
        "htep,phrd->hterd", route, got_out, preferred_element_type=jnp.float32
    )
    pick_parts = jnp.einsum(
        "htep,phx->htex", route, got_lse, preferred_element_type=jnp.float32
    ).reshape(heads_loc, tiles, 2, LANE_ROWS, tile_rows)
    pick_lse = pick_parts[:, :, :, 0] + (pick_parts[:, :, :, 1] + pick_parts[:, :, :, 2])
    keep = valid[..., None]
    top = jnp.maximum(own_lse, jnp.max(jnp.where(keep, pick_lse, own_lse[:, :, None]), axis=2))
    own_w = jnp.exp(own_lse - top)
    pick_w = jnp.exp(jnp.where(keep, pick_lse - top[:, :, None], jnp.float32(-1e30)))
    numer = own_w[..., None] * own_out + jnp.sum(pick_w[..., None] * pick_out, axis=2)
    denom = own_w + jnp.sum(pick_w, axis=2)
    attention = jnp.transpose(numer / denom[..., None], (1, 2, 0, 3)).reshape(
        tokens_here, heads_loc * width
    )
    attention = attention.astype(jnp.bfloat16)
    pair = lax.axis_size("zh")
    mine_zh = lax.axis_index("zh")
    ring = lax.axis_size("y")
    partner = lax.ppermute(attention, "zh", [(0, 1), (1, 0)])
    both = jnp.stack([attention, partner])
    spread = jnp.broadcast_to(both[None], (ring,) + both.shape)
    got_both = lax.all_to_all(spread, "y", split_axis=0, concat_axis=0, tiled=True)
    groups = out_weight.reshape(ring, pair, heads_loc * width, out_weight.shape[1])
    own_w = lax.dynamic_index_in_dim(groups, mine_zh, axis=1, keepdims=False)
    partner_w = lax.dynamic_index_in_dim(groups, 1 - mine_zh, axis=1, keepdims=False)
    projected = jnp.einsum(
        "yrc,ycn->rn", got_both[:, 0], own_w, preferred_element_type=jnp.float32
    ) + jnp.einsum("yrc,ycn->rn", got_both[:, 1], partner_w, preferred_element_type=jnp.float32)
    return projected.astype(jnp.bfloat16)


def solution(mesh):
    ctx_n, head_n = mesh.devices.shape
    split = Mesh(mesh.devices.reshape(ctx_n, head_n // 2, 2), ("ctx", "y", "zh"))
    head = ("y", "zh")
    return jax.shard_map(
        local,
        mesh=split,
        in_specs=(
            P("ctx", head),
            P("ctx", head),
            P("ctx", head),
            P(head, "ctx", None),
            P(None, head),
        ),
        out_specs=P("ctx", head),
        check_vma=False,
    )
```

```python
import functools

import jax
import jax.numpy as jnp
from jax import lax
from jax.experimental import pallas as pl
from jax.experimental.pallas import tpu as pltpu
from jax.sharding import Mesh, PartitionSpec as P

CAP = 2
LANE_ROWS = 4
LSE_ROWS = 16


def split_bf16(x):
    hi = lax.reduce_precision(x, exponent_bits=8, mantissa_bits=7)
    rest = x - hi
    mid = lax.reduce_precision(rest, exponent_bits=8, mantissa_bits=7)
    lo = rest - mid
    return jnp.stack([hi, mid, lo]).astype(jnp.bfloat16)


def join_bf16(parts):
    parts = parts.astype(jnp.float32)
    return parts[0] + (parts[1] + parts[2])


def softmax_pv(scores, vals):
    top = jnp.max(scores, axis=-1)
    prob = jnp.exp(scores - top[..., None])
    total = jnp.sum(prob, axis=-1)
    part = jnp.einsum(
        "hrk,khd->hrd", prob.astype(jnp.bfloat16), vals, preferred_element_type=jnp.float32
    )
    return part / total[..., None], top + jnp.log(total)


def owner_kernel(scale, q_ref, k_ref, v_ref, part_ref):
    groups = q_ref.shape[0]
    slots = q_ref.shape[1]
    rows = q_ref.shape[2]
    width = q_ref.shape[3]
    heads = k_ref.shape[1] // width
    lanes = groups * rows
    nt = (((1,), (1,)), ((), ()))
    tn = (((0,), (0,)), ((), ()))
    tail = part_ref.shape[1] - slots * rows
    part_ref[:, pl.ds(slots * rows, tail)] = jnp.zeros((groups, tail, width), part_ref.dtype)
    owner = lax.broadcasted_iota(jnp.int32, (groups, lanes), 1) // rows
    mask = owner == lax.broadcasted_iota(jnp.int32, (groups, lanes), 0)
    src_lane = lax.broadcasted_iota(jnp.int32, (lanes, width), 0) % rows
    dst_lane = lax.broadcasted_iota(jnp.int32, (lanes, width), 1)
    for j in range(slots):
        cols = pl.ds((j % heads) * width, width)
        q = q_ref[:, j].reshape(lanes, width)
        k = k_ref[:, cols]
        v = v_ref[:, cols]
        s_t = lax.dot_general(k, q, nt, preferred_element_type=jnp.float32) * scale
        top_t = jnp.max(s_t, axis=0, keepdims=True)
        prob_t = jnp.exp(s_t - top_t)
        total_t = jnp.sum(prob_t, axis=0, keepdims=True)
        out_t = lax.dot_general(
            v, prob_t.astype(jnp.bfloat16), tn, preferred_element_type=jnp.float32
        ) / total_t
        part_ref[:, pl.ds(j * rows, rows)] = out_t.T.reshape(groups, rows, width).astype(
            part_ref.dtype
        )
        lse = top_t + jnp.log(total_t)
        hi = lse.astype(jnp.bfloat16)
        rest = lse - hi.astype(jnp.float32)
        mid = rest.astype(jnp.bfloat16)
        lo = (rest - mid.astype(jnp.float32)).astype(jnp.bfloat16)
        packed = jnp.zeros((groups, width), jnp.float32)
        for p, piece in enumerate((hi, mid, lo)):
            spread = jnp.where(mask, jnp.broadcast_to(piece, (groups, lanes)), 0).astype(
                jnp.bfloat16
            )
            place = (dst_lane == src_lane + p * rows).astype(jnp.bfloat16)
            packed = packed + jnp.dot(spread, place, preferred_element_type=jnp.float32)
        part_ref[:, pl.ds(slots * rows + j, 1)] = packed.reshape(groups, 1, width).astype(
            part_ref.dtype
        )


def owner_attention(got, keys, values, scale, extra):
    sources, slots, rows, width = got.shape
    packed = (sources, slots * rows + extra, width)
    return pl.pallas_call(
        functools.partial(owner_kernel, scale),
        grid=(1,),
        in_specs=[
            pl.BlockSpec(got.shape, lambda i: (0, 0, 0, 0)),
            pl.BlockSpec(keys.shape, lambda i: (0, 0)),
            pl.BlockSpec(values.shape, lambda i: (0, 0)),
        ],
        out_specs=pl.BlockSpec(packed, lambda i: (0, 0, 0)),
        out_shape=jax.ShapeDtypeStruct(packed, jnp.bfloat16),
        cost_estimate=pl.CostEstimate(
            flops=6 * sources * slots * rows * keys.shape[0] * width,
            transcendentals=2 * sources * slots * rows * keys.shape[0],
            bytes_accessed=2 * got.size * 2,
        ),
    )(got, keys, values)


def local(queries, keys, values, selected, out_weight):
    heads_loc = selected.shape[0]
    tiles = selected.shape[1]
    tokens_here = queries.shape[0]
    width = queries.shape[1] // heads_loc
    tile_rows = tokens_here // tiles
    sources = lax.axis_size("ctx")
    mine = lax.axis_index("ctx")
    scale = width ** (-0.5)
    quer_three = queries.reshape(tokens_here, heads_loc, width)
    keys_three = keys.reshape(tokens_here, heads_loc, width)
    vals_three = values.reshape(tokens_here, heads_loc, width)

    pos = jnp.arange(tokens_here, dtype=jnp.int32)
    own_scores = (
        jnp.einsum("rhd,khd->hrk", quer_three, keys_three, preferred_element_type=jnp.float32)
        * scale
    )
    own_scores = jnp.where((pos[:, None] >= pos[None, :])[None], own_scores, jnp.float32(-1e30))
    own_out, own_lse = softmax_pv(own_scores, vals_three)
    own_out = own_out.reshape(heads_loc, tiles, tile_rows, width)
    own_lse = own_lse.reshape(heads_loc, tiles, tile_rows)

    picks = selected[:, :, 1:]
    valid = picks != mine
    target = jnp.where(valid, picks, sources)
    onehot = (target[..., None] == jnp.arange(sources, dtype=jnp.int32)).astype(jnp.int32)
    flat_hot = onehot.reshape(heads_loc, tiles * 2, sources)
    before = jnp.cumsum(flat_hot, axis=1) - flat_hot
    slot = jnp.sum(before * flat_hot, axis=-1).reshape(heads_loc, tiles, 2)
    query_src = jnp.transpose(
        quer_three.reshape(tiles, tile_rows, heads_loc, width), (2, 0, 1, 3)
    ).reshape(heads_loc, tiles, tile_rows * width)
    flat_slot = target * CAP + slot
    route = (
        flat_slot[..., None] == jnp.arange(sources * CAP, dtype=jnp.int32)
    ).astype(jnp.bfloat16)
    send_q = jnp.einsum(
        "htep,htx->phx", route, query_src, preferred_element_type=jnp.float32
    ).astype(jnp.bfloat16)
    send_q = send_q.reshape(sources, CAP, heads_loc, tile_rows, width)
    got_rows = lax.all_to_all(send_q, "ctx", split_axis=0, concat_axis=0, tiled=True)

    rows_part = CAP * heads_loc * tile_rows
    extra = -(rows_part + CAP * heads_loc) % 16 + CAP * heads_loc
    back = owner_attention(
        got_rows.reshape(sources, CAP * heads_loc, tile_rows, width), keys, values, scale, extra
    )
    got_back = lax.all_to_all(back, "ctx", split_axis=0, concat_axis=0, tiled=True)
    got_out = got_back[:, :rows_part].reshape(sources * CAP, heads_loc, tile_rows, width)
    got_lse = got_back[:, rows_part : rows_part + CAP * heads_loc].reshape(
        sources * CAP, heads_loc, width
    )
    pick_out = jnp.einsum(
        "htep,phrd->hterd", route, got_out, preferred_element_type=jnp.float32
    )
    pick_parts = jnp.einsum(
        "htep,phx->htex", route, got_lse, preferred_element_type=jnp.float32
    ).reshape(heads_loc, tiles, 2, LANE_ROWS, tile_rows)
    pick_lse = pick_parts[:, :, :, 0] + (pick_parts[:, :, :, 1] + pick_parts[:, :, :, 2])
    keep = valid[..., None]
    top = jnp.maximum(own_lse, jnp.max(jnp.where(keep, pick_lse, own_lse[:, :, None]), axis=2))
    own_w = jnp.exp(own_lse - top)
    pick_w = jnp.exp(jnp.where(keep, pick_lse - top[:, :, None], jnp.float32(-1e30)))
    numer = own_w[..., None] * own_out + jnp.sum(pick_w[..., None] * pick_out, axis=2)
    denom = own_w + jnp.sum(pick_w, axis=2)
    attention = jnp.transpose(numer / denom[..., None], (1, 2, 0, 3)).reshape(
        tokens_here, heads_loc * width
    )
    attention = attention.astype(jnp.bfloat16)
    pair = lax.axis_size("zh")
    mine_zh = lax.axis_index("zh")
    ring = lax.axis_size("y")
    partner = lax.ppermute(attention, "zh", [(0, 1), (1, 0)])
    both = jnp.stack([attention, partner])
    spread = jnp.broadcast_to(both[None], (ring,) + both.shape)
    got_both = lax.all_to_all(spread, "y", split_axis=0, concat_axis=0, tiled=True)
    groups = out_weight.reshape(ring, pair, heads_loc * width, out_weight.shape[1])
    own_w = lax.dynamic_index_in_dim(groups, mine_zh, axis=1, keepdims=False)
    partner_w = lax.dynamic_index_in_dim(groups, 1 - mine_zh, axis=1, keepdims=False)
    projected = jnp.einsum(
        "yrc,ycn->rn", got_both[:, 0], own_w, preferred_element_type=jnp.float32
    ) + jnp.einsum("yrc,ycn->rn", got_both[:, 1], partner_w, preferred_element_type=jnp.float32)
    return projected.astype(jnp.bfloat16)


def solution(mesh):
    ctx_n, head_n = mesh.devices.shape
    split = Mesh(mesh.devices.reshape(ctx_n, head_n // 2, 2), ("ctx", "y", "zh"))
    head = ("y", "zh")
    return jax.shard_map(
        local,
        mesh=split,
        in_specs=(
            P("ctx", head),
            P("ctx", head),
            P("ctx", head),
            P(head, "ctx", None),
            P(None, head),
        ),
        out_specs=P("ctx", head),
        check_vma=False,
    )
```
